512 devices in a mesh: seq: 128 (over z, y, core), tensor: 4 (over x).
Axes of the slice: x: 4, y: 8, z: 8, core: 2. Of those that a mesh axis runs over, the one named last changes fastest.
Arguments:
- hidden_in: bfloat16 [32768, 2048], P('seq', 'tensor'), may hold values from -6 to 6
- norm_gain: bfloat16 [2048], replicated, may hold values from 0.5 to 1.5
- query_weight: bfloat16 [2048, 2048], P(None, 'tensor'), may hold values from -2 to 2
- keyval_weight: bfloat16 [2048, 2048], P(None, 'tensor'), may hold values from -8 to 8
- output_weight: bfloat16 [2048, 2048], P('tensor'), may hold values from -0.125 to 0.125
- segment_ids: int32 [32768], P('seq'), may hold values from -1 to 127, as said below
- request_lengths: int32 [128], replicated, may hold values from 1 to 512, as said below
- request_owner: int32 [128], replicated, may hold values from 0 to 127, each once
- cache_slots: int32 [128], replicated, may hold values from 0 to 1
Outputs:
- attended: bfloat16 [32768, 2048], P('seq', 'tensor')
- kv_cache: bfloat16 [256, 512, 2048], P('seq', None, 'tensor')
The draws below stay inside these ranges and needn't reach their ends.
Inputs may be any that keep to these rules, and one draw needn't show every extreme that they name: `segment_ids`: in the packed stream (position t = i * 128 + s for row i of index s of seq) the requests follow one another in order, request r taking request_lengths[r] consecutive positions from start[r]; positions from 28672 on hold -1. `request_lengths`: they sum to 28672; the largest is exactly 512.
All inputs are finite; a program needn't handle non-finite values.
Results may differ from the reference program's by a relative error of at most 0.012.
The reference program's roundings to bfloat16 on the way count: a program that leaves them out, or rounds other values in their place, can miss the bound.
Values may be sent and summed in bfloat16 or wider, within the bound.
No kernel may reach another device: no remote copies, remote signals or barrier semaphores. Data moves between devices by JAX's collectives and lax.ppermute only.
A program may use at most 64 MiB of HBM per device.

```python
import math
import jax
import jax.numpy as jnp
from jax import lax

D = 2048
HEADS = 8
KV_HEADS = 4
HD = 256
TOK_DEV = 256
SLOTS_DEV = 2
TOKENS = 32768
NREQ = 128
MAXLEN = 512
FILLED = 28672
N_SEQ = 128
N_TENSOR = 4


def packing(key):
    request_index = jnp.arange(NREQ, dtype=jnp.int32)
    longest = jax.random.randint(jax.random.fold_in(key, 21), (), 0, NREQ)
    shares = jax.random.randint(jax.random.fold_in(key, 22), (NREQ,), 4, 8)
    others = request_index != longest
    shares = jnp.where(others, shares, 0)
    spare_tokens = FILLED - MAXLEN - (NREQ - 1)
    extra_tokens = spare_tokens * shares // jnp.sum(shares)
    leftover = spare_tokens - jnp.sum(extra_tokens)
    order_rank = jnp.cumsum(others.astype(jnp.int32)) - 1
    extra_tokens = extra_tokens + ((order_rank < leftover) & others).astype(jnp.int32)
    return jnp.where(others, 1 + extra_tokens, MAXLEN).astype(jnp.int32)


def draw_request_lengths(key, part):
    return packing(key)


def draw_segment_ids(key, part):
    lengths_drawn = packing(key)
    starts = jnp.cumsum(lengths_drawn) - lengths_drawn
    positions = jnp.arange(TOKENS, dtype=jnp.int32)
    stream_seg = jnp.sum((positions[:, None] >= starts[None, :]).astype(jnp.int32), axis=1) - 1
    stream_seg = jnp.where(positions < FILLED, stream_seg, -1)
    return stream_seg.reshape(TOK_DEV, NREQ).T.reshape(TOKENS).astype(jnp.int32)


def query_base(key):
    drawn = jax.random.normal(jax.random.fold_in(key, 31), (D, HEADS * HD), jnp.float32)
    return jnp.clip(drawn, -5.0, 5.0) * (2.0 / math.sqrt(D))


def draw_query_weight(key, part):
    return query_base(key).astype(jnp.bfloat16)


def draw_keyval_weight(key, part):
    fresh = jax.random.normal(jax.random.fold_in(key, 32), (D, KV_HEADS, 2, HD), jnp.float32)
    fresh = jnp.clip(fresh, -5.0, 5.0) * (2.0 / math.sqrt(D))
    return fresh.reshape(D, KV_HEADS * 2 * HD).astype(jnp.bfloat16)


def set_ends(values, key, low, largest):
    dims = values.shape
    index_at = [jax.random.randint(jax.random.fold_in(key, axis), (), 0, dims[axis]) for axis in range(len(dims))]
    values = values.at[tuple(index_at)].set(low)
    longest = dims.index(max(dims))
    index_at[longest] = (index_at[longest] + 1) % dims[longest]
    return values.at[tuple(index_at)].set(largest)


def levels(stream_key, extent, split, least, largest):
    factor_of, own = 1.0, jax.random.fold_in(stream_key, 6)
    for dim, blocks in split:
        heights = jnp.exp(jax.random.uniform(jax.random.fold_in(own, dim), (blocks,), jnp.float32, least / len(split), largest / len(split)))
        factor_of = factor_of * jnp.repeat(heights, extent[dim] // blocks).reshape([-1 if axis == dim else 1 for axis in range(len(extent))])
    return factor_of


def noise(stream_key, dims, width, reach, split=(), kind=jnp.bfloat16):
    values = width * jax.random.normal(stream_key, dims, jnp.float32)
    if split:
        values = values * levels(stream_key, dims, split, -0.22, 0.18)
    return jnp.clip(values, -reach, reach).astype(kind)


def setup_inputs(seed: int = 0) -> dict:
    streams_of = jax.random.split(jax.random.key(seed), 10)
    hidden_in = noise(streams_of[0], (TOKENS, D), 1.0, 6.0, ((0, 128), (1, 4)))
    norm_gain = jnp.clip(jax.random.uniform(streams_of[1], (D,), jnp.float32, 0.5, 1.5), 0.5, 1.5).astype(jnp.bfloat16)
    query_weight = draw_query_weight(jax.random.fold_in(streams_of[9], 71), 0)
    keyval_weight = draw_keyval_weight(jax.random.fold_in(streams_of[9], 71), 0)
    output_weight = noise(streams_of[4], (HEADS * HD, D), (HEADS * HD) ** -0.5, 0.125, ((0, 4),))
    segment_ids = draw_segment_ids(jax.random.fold_in(streams_of[9], 71), 0)
    request_lengths = draw_request_lengths(jax.random.fold_in(streams_of[9], 71), 0)
    request_owner = jax.random.permutation(streams_of[7], NREQ).astype(jnp.int32)
    cache_slots = set_ends(jax.random.randint(streams_of[8], (NREQ,), 0, SLOTS_DEV), jax.random.fold_in(streams_of[8], 1), 0, SLOTS_DEV - 1).astype(jnp.int32)
    return {"hidden_in": hidden_in, "norm_gain": norm_gain, "query_weight": query_weight, "keyval_weight": keyval_weight, "output_weight": output_weight, "segment_ids": segment_ids, "request_lengths": request_lengths, "request_owner": request_owner, "cache_slots": cache_slots}


EPSILON = 1e-06
ROPE_BASE = 1000042.0

def rotate_rows(values, head_size):
    row_count = values.shape[0]
    shaped = values.reshape(row_count, -1, head_size)
    half_size = head_size // 2
    frequency = ROPE_BASE ** (jnp.arange(half_size, dtype=jnp.float32) * (-2.0 / head_size))
    angles = jnp.arange(row_count, dtype=jnp.float32)[:, None] * frequency[None, :]
    cosine_table = jnp.cos(angles)[:, None, :]
    sine_table = jnp.sin(angles)[:, None, :]
    first_half = shaped[..., :half_size]
    second_half = shaped[..., half_size:]
    turned = jnp.concatenate([first_half * cosine_table - second_half * sine_table, second_half * cosine_table + first_half * sine_table], axis=-1)
    return turned.reshape(values.shape)

def normalize(rows_in, gain):
    widened = rows_in.astype(jnp.float32)
    inverse_rms = lax.rsqrt(lax.optimization_barrier(jnp.mean(widened * widened, axis=-1, keepdims=True)) + EPSILON)
    return (widened * inverse_rms * gain.astype(jnp.float32)).astype(jnp.bfloat16)

def attend(query_block, start_row, key_rows, value_rows, length):
    row_count = query_block.shape[0]
    scores = jnp.dot(query_block, key_rows.T, preferred_element_type=jnp.float32) * key_rows.shape[1] ** (-0.5)
    query_pos = start_row + jnp.arange(row_count, dtype=jnp.int32)[:, None]
    key_pos = jnp.arange(key_rows.shape[0], dtype=jnp.int32)[None, :]
    allowed = (key_pos <= query_pos) & (key_pos < length)
    scores = jnp.where(allowed, scores, -jnp.inf)
    row_top = lax.optimization_barrier(jnp.max(scores, axis=-1, keepdims=True))
    powered = jnp.exp(scores - row_top)
    weights = (powered / lax.optimization_barrier(jnp.sum(powered, axis=-1, keepdims=True))).astype(jnp.bfloat16)
    return jnp.dot(weights, value_rows, preferred_element_type=jnp.float32).astype(jnp.bfloat16)

def to_stream(values):
    shaped = values.reshape((N_SEQ, TOK_DEV) + values.shape[1:])
    return jnp.swapaxes(shaped, 0, 1).reshape(values.shape)

def to_packed(values):
    shaped = values.reshape((TOK_DEV, N_SEQ) + values.shape[1:])
    return jnp.swapaxes(shaped, 0, 1).reshape(values.shape)

def reference(hidden_in, norm_gain, query_weight, keyval_weight, output_weight, segment_ids, request_lengths, request_owner, cache_slots):
    stream_rows = to_stream(hidden_in)
    stream_seg = to_stream(segment_ids)
    normed = normalize(stream_rows, norm_gain)
    queries = jnp.dot(normed, query_weight, preferred_element_type=jnp.float32)
    keyvals = jnp.dot(normed, keyval_weight, preferred_element_type=jnp.float32)
    padded_query = jnp.concatenate([queries, jnp.zeros((MAXLEN, queries.shape[1]), jnp.float32)], axis=0)
    padded_keyval = jnp.concatenate([keyvals, jnp.zeros((MAXLEN, keyvals.shape[1]), jnp.float32)], axis=0)
    padded_seg = jnp.concatenate([stream_seg, jnp.full((MAXLEN,), -1, jnp.int32)], axis=0)
    starts = (jnp.cumsum(request_lengths) - request_lengths).astype(jnp.int32)

    def one_request(request):
        start_pos = starts[request]
        length = request_lengths[request]
        live_rows = lax.dynamic_slice_in_dim(padded_seg, start_pos, MAXLEN, 0) == request
        query_window = jnp.where(live_rows[:, None], lax.dynamic_slice_in_dim(padded_query, start_pos, MAXLEN, 0), 0.0)
        keyval_window = jnp.where(live_rows[:, None], lax.dynamic_slice_in_dim(padded_keyval, start_pos, MAXLEN, 0), 0.0)
        rotated_query = rotate_rows(query_window, HD).astype(jnp.bfloat16)
        keyval_shaped = keyval_window.reshape(MAXLEN, KV_HEADS, 2, HD)
        rotated_keys = rotate_rows(keyval_shaped[:, :, 0, :].reshape(MAXLEN, KV_HEADS * HD), HD).reshape(MAXLEN, KV_HEADS, 1, HD)
        cached = jnp.concatenate([rotated_keys, keyval_shaped[:, :, 1:, :]], axis=2).reshape(MAXLEN, 2 * KV_HEADS * HD).astype(jnp.bfloat16)
        head_outputs = []
        for head_index in range(HEADS):
            group_index = head_index // (HEADS // KV_HEADS)
            head_keys = cached[:, 2 * group_index * HD:(2 * group_index + 1) * HD]
            head_values = cached[:, (2 * group_index + 1) * HD:(2 * group_index + 2) * HD]
            head_outputs.append(attend(rotated_query[:, head_index * HD:(head_index + 1) * HD], 0, head_keys, head_values, length))
        return (jnp.concatenate(head_outputs, axis=1), cached)
    attention_windows, cached_all = lax.map(one_request, jnp.arange(NREQ, dtype=jnp.int32))
    safe_segment = jnp.maximum(stream_seg, 0)
    offset = jnp.arange(TOKENS, dtype=jnp.int32) - starts[safe_segment]
    usable = (stream_seg >= 0) & (offset >= 0) & (offset < MAXLEN)
    flat_index = (safe_segment * MAXLEN + jnp.clip(offset, 0, MAXLEN - 1)).astype(jnp.int32)
    attention_rows = jnp.where(usable[:, None], attention_windows.reshape(NREQ * MAXLEN, -1)[flat_index], jnp.zeros((), jnp.bfloat16))
    part_width = HEADS * HD // N_TENSOR
    running_sum = jnp.zeros((TOKENS, D), jnp.float32)
    for part_index in range(N_TENSOR):
        partial_term = jnp.dot(attention_rows[:, part_index * part_width:(part_index + 1) * part_width], output_weight[part_index * part_width:(part_index + 1) * part_width, :], preferred_element_type=jnp.float32)
        running_sum = running_sum + lax.optimization_barrier(partial_term.astype(jnp.bfloat16)).astype(jnp.float32)
    attended = to_packed(running_sum.astype(jnp.bfloat16))
    cache_index = (request_owner * SLOTS_DEV + cache_slots).astype(jnp.int32)
    cache_table = jnp.zeros((NREQ * SLOTS_DEV, MAXLEN, 2 * KV_HEADS * HD), jnp.bfloat16).at[cache_index].set(cached_all)
    return (attended, cache_table)
```

```python
import jax
import jax.numpy as jnp
from jax import lax
from jax.sharding import PartitionSpec as P

HEADS = 8
KV_HEADS = 4
HD = 256
SLOTS_DEV = 2
MAXLEN = 512


EPSILON = 1e-06
ROPE_BASE = 1000042.0
CHUNKS = 2


def rotate_rows(values, head_size, first_pos):
    row_count = values.shape[0]
    shaped = values.reshape(row_count, -1, head_size)
    half_size = head_size // 2
    frequency = ROPE_BASE ** (jnp.arange(half_size, dtype=jnp.float32) * (-2.0 / head_size))
    positions = (first_pos + jnp.arange(row_count, dtype=jnp.int32)).astype(jnp.float32)
    angles = positions[:, None] * frequency[None, :]
    cosine_table = jnp.cos(angles)[:, None, :]
    sine_table = jnp.sin(angles)[:, None, :]
    first_half = shaped[..., :half_size]
    second_half = shaped[..., half_size:]
    turned = jnp.concatenate(
        [
            first_half * cosine_table - second_half * sine_table,
            second_half * cosine_table + first_half * sine_table,
        ],
        axis=-1,
    )
    return turned.reshape(values.shape)


def normalize(rows_in, gain):
    widened = rows_in.astype(jnp.float32)
    inverse_rms = lax.rsqrt(jnp.mean(widened * widened, axis=-1, keepdims=True) + EPSILON)
    return (widened * inverse_rms * gain.astype(jnp.float32)).astype(jnp.bfloat16)


def attend(query_block, start_row, key_rows, value_rows, length):
    row_count = query_block.shape[0]
    scores = jnp.dot(query_block, key_rows.T, preferred_element_type=jnp.float32) * key_rows.shape[
        1
    ] ** (-0.5)
    query_pos = start_row + jnp.arange(row_count, dtype=jnp.int32)[:, None]
    key_pos = jnp.arange(key_rows.shape[0], dtype=jnp.int32)[None, :]
    allowed = (key_pos <= query_pos) & (key_pos < length)
    scores = jnp.where(allowed, scores, -jnp.inf)
    row_top = jnp.max(scores, axis=-1, keepdims=True)
    powered = jnp.exp(scores - row_top)
    weights = (powered / jnp.sum(powered, axis=-1, keepdims=True)).astype(jnp.bfloat16)
    return jnp.dot(weights, value_rows, preferred_element_type=jnp.float32).astype(jnp.bfloat16)


def to_request(received, shift_by):
    rolled = jnp.roll(received, -shift_by, axis=0)
    return jnp.swapaxes(rolled, 0, 1).reshape(-1, received.shape[2])


def from_request(request_rows, shift_by, source_count):
    shaped = request_rows.reshape(-1, source_count, request_rows.shape[1])
    return jnp.roll(jnp.swapaxes(shaped, 0, 1), shift_by, axis=0)


def windows(values, first, count):
    return jax.vmap(lambda at: lax.dynamic_slice_in_dim(values, at, count, 0))(first)


def body(
    hidden_in,
    norm_gain,
    query_weight,
    keyval_weight,
    output_weight,
    segment_ids,
    request_lengths,
    request_owner,
    cache_slots,
):
    source_count = lax.axis_size("seq")
    source_pos = lax.axis_index("seq")
    local_rows = hidden_in.shape[0]
    capacity = MAXLEN // source_count
    chunk_slots = capacity // CHUNKS
    chunk_rows = chunk_slots * source_count
    request_ids = jnp.arange(source_count, dtype=jnp.int32)
    starts = jnp.cumsum(request_lengths) - request_lengths
    first_row = jnp.maximum((starts - source_pos + source_count - 1) // source_count, 0)
    owner_match = request_owner[None, :] == request_ids[:, None]
    owned_by = jnp.sum(jnp.where(owner_match, request_ids[None, :], 0), axis=1)
    send_first = jnp.sum(jnp.where(owner_match, first_row[None, :], 0), axis=1)
    row_index = send_first[:, None] + jnp.arange(capacity, dtype=jnp.int32)[None, :]
    seg_windows = windows(segment_ids, send_first, capacity)
    live_send = (row_index < local_rows) & (seg_windows == owned_by[:, None])
    owned_request = jnp.sum(jnp.where(request_owner == source_pos, request_ids, 0))
    own_match = request_ids == owned_request
    own_start = jnp.sum(jnp.where(own_match, starts, 0))
    own_length = jnp.sum(jnp.where(own_match, request_lengths, 0))
    own_slot = jnp.sum(jnp.where(own_match, cache_slots, 0))
    shift_by = own_start % source_count
    picked = jnp.where(
        live_send[:, :, None], windows(hidden_in, send_first, capacity), jnp.zeros((), jnp.bfloat16)
    )
    head_count = query_weight.shape[1] // HD
    per_group = HEADS // KV_HEADS
    block_count = keyval_weight.shape[1] // HD
    key_chunks = []
    value_chunks = []
    cached_chunks = []
    returned_chunks = []
    for chunk in range(CHUNKS):
        chunk_first = chunk * chunk_rows
        arrived = lax.all_to_all(
            picked[:, chunk * chunk_slots : (chunk + 1) * chunk_slots],
            "seq",
            split_axis=0,
            concat_axis=0,
            tiled=True,
        )
        narrow_rows = to_request(arrived, shift_by)
        full_rows = lax.all_gather(narrow_rows, "tensor", axis=1, tiled=True)
        normed = normalize(full_rows, norm_gain)
        queries = jnp.dot(normed, query_weight, preferred_element_type=jnp.float32)
        keyvals = jnp.dot(normed, keyval_weight, preferred_element_type=jnp.float32)
        rotated_query = rotate_rows(queries, HD, chunk_first).astype(jnp.bfloat16)
        own_blocks = []
        for block_index in range(block_count):
            plain_block = keyvals[:, block_index * HD : (block_index + 1) * HD]
            if block_index % 2 == 0:
                own_blocks.append(rotate_rows(plain_block, HD, chunk_first).astype(jnp.bfloat16))
            else:
                own_blocks.append(plain_block.astype(jnp.bfloat16))
        own_cached = jnp.concatenate(own_blocks, axis=1)
        cached_chunks.append(own_cached)
        key_chunks.append(own_cached[:, 0:HD])
        value_chunks.append(own_cached[:, HD : 2 * HD])
        key_rows = jnp.concatenate(key_chunks, axis=0)
        value_rows = jnp.concatenate(value_chunks, axis=0)
        head_outputs = []
        for head_index in range(head_count):
            head_outputs.append(
                attend(
                    rotated_query[:, head_index * HD : (head_index + 1) * HD],
                    chunk_first,
                    key_rows,
                    value_rows,
                    own_length,
                )
            )
        attention_rows = jnp.concatenate(head_outputs, axis=1)
        outgoing = from_request(attention_rows, shift_by, source_count)
        returned_chunks.append(
            lax.all_to_all(outgoing, "seq", split_axis=0, concat_axis=0, tiled=True)
        )
    returned = jnp.concatenate(returned_chunks, axis=1)
    segment_match = segment_ids[:, None] == request_ids[None, :]
    row_owner = jnp.sum(jnp.where(segment_match, request_owner[None, :], 0), axis=1)
    row_first = jnp.sum(jnp.where(segment_match, first_row[None, :], 0), axis=1)
    slot_pos = jnp.arange(local_rows, dtype=jnp.int32) - row_first
    usable = (segment_ids >= 0) & (slot_pos >= 0) & (slot_pos < capacity)
    flat_index = row_owner * capacity + jnp.clip(slot_pos, 0, capacity - 1)
    flattened = returned.reshape(-1, returned.shape[2])
    local_attention = jnp.where(usable[:, None], flattened[flat_index], jnp.zeros((), returned.dtype))
    partial_sum = jnp.dot(local_attention, output_weight, preferred_element_type=jnp.float32)
    attended = lax.psum_scatter(
        partial_sum.astype(jnp.bfloat16), "tensor", scatter_dimension=1, tiled=True
    )
    all_cached = jnp.concatenate(cached_chunks, axis=0)
    slot_ids = jnp.arange(SLOTS_DEV, dtype=jnp.int32)
    cache_table = jnp.where(
        (slot_ids == own_slot)[:, None, None], all_cached[None], jnp.zeros((), jnp.bfloat16)
    )
    return (attended, cache_table)


def solution(mesh):
    in_specs = (
        P("seq", "tensor"),
        P(),
        P(None, "tensor"),
        P(None, "tensor"),
        P("tensor", None),
        P("seq"),
        P(),
        P(),
        P(),
    )
    out_specs = (P("seq", "tensor"), P("seq", None, "tensor"))
    return jax.shard_map(body, mesh=mesh, in_specs=in_specs, out_specs=out_specs, check_vma=False)
```

```python
import jax
import jax.numpy as jnp
from jax import lax
from jax.sharding import PartitionSpec as P

HEADS = 8
KV_HEADS = 4
HD = 256
SLOTS_DEV = 2
MAXLEN = 512


EPSILON = 1e-06
ROPE_BASE = 1000042.0
CHUNKS = 1


def rotate_rows(values, head_size, first_pos):
    row_count = values.shape[0]
    shaped = values.reshape(row_count, -1, head_size)
    half_size = head_size // 2
    frequency = ROPE_BASE ** (jnp.arange(half_size, dtype=jnp.float32) * (-2.0 / head_size))
    positions = (first_pos + jnp.arange(row_count, dtype=jnp.int32)).astype(jnp.float32)
    angles = positions[:, None] * frequency[None, :]
    cosine_table = jnp.cos(angles)[:, None, :]
    sine_table = jnp.sin(angles)[:, None, :]
    first_half = shaped[..., :half_size]
    second_half = shaped[..., half_size:]
    turned = jnp.concatenate(
        [
            first_half * cosine_table - second_half * sine_table,
            second_half * cosine_table + first_half * sine_table,
        ],
        axis=-1,
    )
    return turned.reshape(values.shape)


def normalize(rows_in, gain):
    widened = rows_in.astype(jnp.float32)
    inverse_rms = lax.rsqrt(jnp.mean(widened * widened, axis=-1, keepdims=True) + EPSILON)
    return (widened * inverse_rms * gain.astype(jnp.float32)).astype(jnp.bfloat16)


def attend(query_block, start_row, key_rows, value_rows, length):
    row_count = query_block.shape[0]
    scores = jnp.dot(query_block, key_rows.T, preferred_element_type=jnp.float32) * key_rows.shape[
        1
    ] ** (-0.5)
    query_pos = start_row + jnp.arange(row_count, dtype=jnp.int32)[:, None]
    key_pos = jnp.arange(key_rows.shape[0], dtype=jnp.int32)[None, :]
    allowed = (key_pos <= query_pos) & (key_pos < length)
    scores = jnp.where(allowed, scores, -jnp.inf)
    row_top = jnp.max(scores, axis=-1, keepdims=True)
    powered = jnp.exp(scores - row_top)
    weights = (powered / jnp.sum(powered, axis=-1, keepdims=True)).astype(jnp.bfloat16)
    return jnp.dot(weights, value_rows, preferred_element_type=jnp.float32).astype(jnp.bfloat16)


def to_request(received, shift_by):
    rolled = jnp.roll(received, -shift_by, axis=0)
    return jnp.swapaxes(rolled, 0, 1).reshape(-1, received.shape[2])


def from_request(request_rows, shift_by, source_count):
    shaped = request_rows.reshape(-1, source_count, request_rows.shape[1])
    return jnp.roll(jnp.swapaxes(shaped, 0, 1), shift_by, axis=0)


def body(
    hidden_in,
    norm_gain,
    query_weight,
    keyval_weight,
    output_weight,
    segment_ids,
    request_lengths,
    request_owner,
    cache_slots,
):
    source_count = lax.axis_size("seq")
    source_pos = lax.axis_index("seq")
    local_rows = hidden_in.shape[0]
    capacity = MAXLEN // source_count
    chunk_slots = capacity // CHUNKS
    chunk_rows = chunk_slots * source_count
    request_ids = jnp.arange(source_count, dtype=jnp.int32)
    starts = jnp.cumsum(request_lengths) - request_lengths
    first_row = jnp.maximum((starts - source_pos + source_count - 1) // source_count, 0)
    owner_match = request_owner[None, :] == request_ids[:, None]
    owned_by = jnp.sum(jnp.where(owner_match, request_ids[None, :], 0), axis=1)
    send_first = jnp.sum(jnp.where(owner_match, first_row[None, :], 0), axis=1)
    row_index = send_first[:, None] + jnp.arange(capacity, dtype=jnp.int32)[None, :]
    safe_index = jnp.minimum(row_index, local_rows - 1)
    live_send = (row_index < local_rows) & (segment_ids[safe_index] == owned_by[:, None])
    owned_request = jnp.sum(jnp.where(request_owner == source_pos, request_ids, 0))
    own_match = request_ids == owned_request
    own_start = jnp.sum(jnp.where(own_match, starts, 0))
    own_length = jnp.sum(jnp.where(own_match, request_lengths, 0))
    own_slot = jnp.sum(jnp.where(own_match, cache_slots, 0))
    shift_by = own_start % source_count
    picked = jnp.where(live_send[:, :, None], hidden_in[safe_index], jnp.zeros((), jnp.bfloat16))
    head_count = query_weight.shape[1] // HD
    per_group = HEADS // KV_HEADS
    block_count = keyval_weight.shape[1] // HD
    key_chunks = []
    value_chunks = []
    cached_chunks = []
    returned_chunks = []
    for chunk in range(CHUNKS):
        chunk_first = chunk * chunk_rows
        arrived = lax.all_to_all(
            picked[:, chunk * chunk_slots : (chunk + 1) * chunk_slots],
            "seq",
            split_axis=0,
            concat_axis=0,
            tiled=True,
        )
        narrow_rows = to_request(arrived, shift_by)
        full_rows = lax.all_gather(narrow_rows, "tensor", axis=1, tiled=True)
        normed = normalize(full_rows, norm_gain)
        queries = jnp.dot(normed, query_weight, preferred_element_type=jnp.float32)
        keyvals = jnp.dot(normed, keyval_weight, preferred_element_type=jnp.float32)
        rotated_query = rotate_rows(queries, HD, chunk_first).astype(jnp.bfloat16)
        own_blocks = []
        for block_index in range(block_count):
            plain_block = keyvals[:, block_index * HD : (block_index + 1) * HD]
            if block_index % 2 == 0:
                own_blocks.append(rotate_rows(plain_block, HD, chunk_first).astype(jnp.bfloat16))
            else:
                own_blocks.append(plain_block.astype(jnp.bfloat16))
        own_cached = jnp.concatenate(own_blocks, axis=1)
        cached_chunks.append(own_cached)
        key_chunks.append(own_cached[:, 0:HD])
        value_chunks.append(own_cached[:, HD : 2 * HD])
        key_rows = jnp.concatenate(key_chunks, axis=0)
        value_rows = jnp.concatenate(value_chunks, axis=0)
        head_outputs = []
        for head_index in range(head_count):
            head_outputs.append(
                attend(
                    rotated_query[:, head_index * HD : (head_index + 1) * HD],
                    chunk_first,
                    key_rows,
                    value_rows,
                    own_length,
                )
            )
        attention_rows = jnp.concatenate(head_outputs, axis=1)
        outgoing = from_request(attention_rows, shift_by, source_count)
        returned_chunks.append(
            lax.all_to_all(outgoing, "seq", split_axis=0, concat_axis=0, tiled=True)
        )
    returned = jnp.concatenate(returned_chunks, axis=1)
    segment_match = segment_ids[:, None] == request_ids[None, :]
    row_owner = jnp.sum(jnp.where(segment_match, request_owner[None, :], 0), axis=1)
    row_first = jnp.sum(jnp.where(segment_match, first_row[None, :], 0), axis=1)
    slot_pos = jnp.arange(local_rows, dtype=jnp.int32) - row_first
    usable = (segment_ids >= 0) & (slot_pos >= 0) & (slot_pos < capacity)
    flat_index = row_owner * capacity + jnp.clip(slot_pos, 0, capacity - 1)
    flattened = returned.reshape(-1, returned.shape[2])
    local_attention = jnp.where(usable[:, None], flattened[flat_index], jnp.zeros((), returned.dtype))
    partial_sum = jnp.dot(local_attention, output_weight, preferred_element_type=jnp.float32)
    attended = lax.psum_scatter(
        partial_sum.astype(jnp.bfloat16), "tensor", scatter_dimension=1, tiled=True
    )
    all_cached = jnp.concatenate(cached_chunks, axis=0)
    slot_ids = jnp.arange(SLOTS_DEV, dtype=jnp.int32)
    cache_table = jnp.where(
        (slot_ids == own_slot)[:, None, None], all_cached[None], jnp.zeros((), jnp.bfloat16)
    )
    return (attended, cache_table)


def solution(mesh):
    in_specs = (
        P("seq", "tensor"),
        P(),
        P(None, "tensor"),
        P(None, "tensor"),
        P("tensor", None),
        P("seq"),
        P(),
        P(),
        P(),
    )
    out_specs = (P("seq", "tensor"), P("seq", None, "tensor"))
    return jax.shard_map(body, mesh=mesh, in_specs=in_specs, out_specs=out_specs, check_vma=False)
```

```python
import jax
import jax.numpy as jnp
from jax import lax
from jax.sharding import Mesh, PartitionSpec as P

HEADS = 8
KV_HEADS = 4
HD = 256
SLOTS_DEV = 2
MAXLEN = 512


EPSILON = 1e-06
ROPE_BASE = 1000042.0
CHUNKS = 1
LO_SIZE = 16


def rotate_rows(values, head_size, first_pos):
    row_count = values.shape[0]
    shaped = values.reshape(row_count, -1, head_size)
    half_size = head_size // 2
    frequency = ROPE_BASE ** (jnp.arange(half_size, dtype=jnp.float32) * (-2.0 / head_size))
    positions = (first_pos + jnp.arange(row_count, dtype=jnp.int32)).astype(jnp.float32)
    angles = positions[:, None] * frequency[None, :]
    cosine_table = jnp.cos(angles)[:, None, :]
    sine_table = jnp.sin(angles)[:, None, :]
    first_half = shaped[..., :half_size]
    second_half = shaped[..., half_size:]
    turned = jnp.concatenate(
        [
            first_half * cosine_table - second_half * sine_table,
            second_half * cosine_table + first_half * sine_table,
        ],
        axis=-1,
    )
    return turned.reshape(values.shape)


def normalize(rows_in, gain):
    widened = rows_in.astype(jnp.float32)
    inverse_rms = lax.rsqrt(jnp.mean(widened * widened, axis=-1, keepdims=True) + EPSILON)
    return (widened * inverse_rms * gain.astype(jnp.float32)).astype(jnp.bfloat16)


def attend(query_block, start_row, key_rows, value_rows, length):
    row_count = query_block.shape[0]
    scores = jnp.dot(query_block, key_rows.T, preferred_element_type=jnp.float32) * key_rows.shape[
        1
    ] ** (-0.5)
    query_pos = start_row + jnp.arange(row_count, dtype=jnp.int32)[:, None]
    key_pos = jnp.arange(key_rows.shape[0], dtype=jnp.int32)[None, :]
    allowed = (key_pos <= query_pos) & (key_pos < length)
    scores = jnp.where(allowed, scores, -jnp.inf)
    row_top = jnp.max(scores, axis=-1, keepdims=True)
    powered = jnp.exp(scores - row_top)
    weights = (powered / jnp.sum(powered, axis=-1, keepdims=True)).astype(jnp.bfloat16)
    return jnp.dot(weights, value_rows, preferred_element_type=jnp.float32).astype(jnp.bfloat16)


SEQ_AXES = ("seq_hi", "seq_lo")


def seq_all_to_all(values):
    hi = lax.axis_size("seq_hi")
    lo = lax.axis_size("seq_lo")
    shaped = values.reshape((hi, lo) + values.shape[1:])
    shaped = lax.all_to_all(shaped, "seq_lo", split_axis=1, concat_axis=1, tiled=True)
    shaped = lax.all_to_all(shaped, "seq_hi", split_axis=0, concat_axis=0, tiled=True)
    return shaped.reshape(values.shape)


def to_request(received, shift_by):
    rolled = jnp.roll(received, -shift_by, axis=0)
    return jnp.swapaxes(rolled, 0, 1).reshape(-1, received.shape[2])


def from_request(request_rows, shift_by, source_count):
    shaped = request_rows.reshape(-1, source_count, request_rows.shape[1])
    return jnp.roll(jnp.swapaxes(shaped, 0, 1), shift_by, axis=0)


def body(
    hidden_in,
    norm_gain,
    query_weight,
    keyval_weight,
    output_weight,
    segment_ids,
    request_lengths,
    request_owner,
    cache_slots,
):
    source_count = lax.axis_size(SEQ_AXES)
    source_pos = lax.axis_index(SEQ_AXES)
    local_rows = hidden_in.shape[0]
    capacity = MAXLEN // source_count
    chunk_slots = capacity // CHUNKS
    chunk_rows = chunk_slots * source_count
    request_ids = jnp.arange(source_count, dtype=jnp.int32)
    starts = jnp.cumsum(request_lengths) - request_lengths
    first_row = jnp.maximum((starts - source_pos + source_count - 1) // source_count, 0)
    owner_match = request_owner[None, :] == request_ids[:, None]
    owned_by = jnp.sum(jnp.where(owner_match, request_ids[None, :], 0), axis=1)
    send_first = jnp.sum(jnp.where(owner_match, first_row[None, :], 0), axis=1)
    row_index = send_first[:, None] + jnp.arange(capacity, dtype=jnp.int32)[None, :]
    safe_index = jnp.minimum(row_index, local_rows - 1)
    live_send = (row_index < local_rows) & (segment_ids[safe_index] == owned_by[:, None])
    owned_request = jnp.sum(jnp.where(request_owner == source_pos, request_ids, 0))
    own_match = request_ids == owned_request
    own_start = jnp.sum(jnp.where(own_match, starts, 0))
    own_length = jnp.sum(jnp.where(own_match, request_lengths, 0))
    own_slot = jnp.sum(jnp.where(own_match, cache_slots, 0))
    shift_by = own_start % source_count
    picked = jnp.where(live_send[:, :, None], hidden_in[safe_index], jnp.zeros((), jnp.bfloat16))
    head_count = query_weight.shape[1] // HD
    per_group = HEADS // KV_HEADS
    block_count = keyval_weight.shape[1] // HD
    key_chunks = []
    value_chunks = []
    cached_chunks = []
    returned_chunks = []
    for chunk in range(CHUNKS):
        chunk_first = chunk * chunk_rows
        arrived = seq_all_to_all(picked[:, chunk * chunk_slots : (chunk + 1) * chunk_slots])
        narrow_rows = to_request(arrived, shift_by)
        full_rows = lax.all_gather(narrow_rows, "tensor", axis=1, tiled=True)
        normed = normalize(full_rows, norm_gain)
        queries = jnp.dot(normed, query_weight, preferred_element_type=jnp.float32)
        keyvals = jnp.dot(normed, keyval_weight, preferred_element_type=jnp.float32)
        rotated_query = rotate_rows(queries, HD, chunk_first).astype(jnp.bfloat16)
        own_blocks = []
        for block_index in range(block_count):
            plain_block = keyvals[:, block_index * HD : (block_index + 1) * HD]
            if block_index % 2 == 0:
                own_blocks.append(rotate_rows(plain_block, HD, chunk_first).astype(jnp.bfloat16))
            else:
                own_blocks.append(plain_block.astype(jnp.bfloat16))
        own_cached = jnp.concatenate(own_blocks, axis=1)
        cached_chunks.append(own_cached)
        key_chunks.append(own_cached[:, 0:HD])
        value_chunks.append(own_cached[:, HD : 2 * HD])
        key_rows = jnp.concatenate(key_chunks, axis=0)
        value_rows = jnp.concatenate(value_chunks, axis=0)
        head_outputs = []
        for head_index in range(head_count):
            head_outputs.append(
                attend(
                    rotated_query[:, head_index * HD : (head_index + 1) * HD],
                    chunk_first,
                    key_rows,
                    value_rows,
                    own_length,
                )
            )
        attention_rows = jnp.concatenate(head_outputs, axis=1)
        outgoing = from_request(attention_rows, shift_by, source_count)
        returned_chunks.append(seq_all_to_all(outgoing))
    returned = jnp.concatenate(returned_chunks, axis=1)
    segment_match = segment_ids[:, None] == request_ids[None, :]
    row_owner = jnp.sum(jnp.where(segment_match, request_owner[None, :], 0), axis=1)
    row_first = jnp.sum(jnp.where(segment_match, first_row[None, :], 0), axis=1)
    slot_pos = jnp.arange(local_rows, dtype=jnp.int32) - row_first
    usable = (segment_ids >= 0) & (slot_pos >= 0) & (slot_pos < capacity)
    flat_index = row_owner * capacity + jnp.clip(slot_pos, 0, capacity - 1)
    flattened = returned.reshape(-1, returned.shape[2])
    local_attention = jnp.where(usable[:, None], flattened[flat_index], jnp.zeros((), returned.dtype))
    partial_sum = jnp.dot(local_attention, output_weight, preferred_element_type=jnp.float32)
    attended = lax.psum_scatter(
        partial_sum.astype(jnp.bfloat16), "tensor", scatter_dimension=1, tiled=True
    )
    all_cached = jnp.concatenate(cached_chunks, axis=0)
    slot_ids = jnp.arange(SLOTS_DEV, dtype=jnp.int32)
    cache_table = jnp.where(
        (slot_ids == own_slot)[:, None, None], all_cached[None], jnp.zeros((), jnp.bfloat16)
    )
    return (attended, cache_table)


def solution(mesh):
    seq_size = mesh.shape["seq"]
    lo_size = LO_SIZE if seq_size % LO_SIZE == 0 else seq_size
    split_mesh = Mesh(
        mesh.devices.reshape(seq_size // lo_size, lo_size, mesh.shape["tensor"]),
        SEQ_AXES + ("tensor",),
    )
    in_specs = (
        P(SEQ_AXES, "tensor"),
        P(),
        P(None, "tensor"),
        P(None, "tensor"),
        P("tensor", None),
        P(SEQ_AXES),
        P(),
        P(),
        P(),
    )
    out_specs = (P(SEQ_AXES, "tensor"), P(SEQ_AXES, None, "tensor"))
    return jax.shard_map(body, mesh=split_mesh, in_specs=in_specs, out_specs=out_specs, check_vma=False)
```

```python
import jax
import jax.numpy as jnp
from jax import lax
from jax.sharding import PartitionSpec as P

HEADS = 8
KV_HEADS = 4
HD = 256
SLOTS_DEV = 2
MAXLEN = 512


EPSILON = 1e-06
ROPE_BASE = 1000042.0
CHUNKS = 1


def rotate_rows(values, head_size, first_pos):
    row_count = values.shape[0]
    shaped = values.reshape(row_count, -1, head_size)
    half_size = head_size // 2
    frequency = ROPE_BASE ** (jnp.arange(half_size, dtype=jnp.float32) * (-2.0 / head_size))
    positions = (first_pos + jnp.arange(row_count, dtype=jnp.int32)).astype(jnp.float32)
    angles = positions[:, None] * frequency[None, :]
    cosine_table = jnp.cos(angles)[:, None, :]
    sine_table = jnp.sin(angles)[:, None, :]
    first_half = shaped[..., :half_size]
    second_half = shaped[..., half_size:]
    turned = jnp.concatenate(
        [
            first_half * cosine_table - second_half * sine_table,
            second_half * cosine_table + first_half * sine_table,
        ],
        axis=-1,
    )
    return turned.reshape(values.shape)


def normalize(rows_in, gain):
    widened = rows_in.astype(jnp.float32)
    inverse_rms = lax.rsqrt(jnp.mean(widened * widened, axis=-1, keepdims=True) + EPSILON)
    return (widened * inverse_rms * gain.astype(jnp.float32)).astype(jnp.bfloat16)


def attend(query_block, start_row, key_rows, value_rows, length):
    row_count = query_block.shape[0]
    scores = jnp.dot(query_block, key_rows.T, preferred_element_type=jnp.float32) * key_rows.shape[
        1
    ] ** (-0.5)
    query_pos = start_row + jnp.arange(row_count, dtype=jnp.int32)[:, None]
    key_pos = jnp.arange(key_rows.shape[0], dtype=jnp.int32)[None, :]
    allowed = (key_pos <= query_pos) & (key_pos < length)
    scores = jnp.where(allowed, scores, -jnp.inf)
    row_top = jnp.max(scores, axis=-1, keepdims=True)
    powered = jnp.exp(scores - row_top)
    weights = (powered / jnp.sum(powered, axis=-1, keepdims=True)).astype(jnp.bfloat16)
    return jnp.dot(weights, value_rows, preferred_element_type=jnp.float32).astype(jnp.bfloat16)


def to_request(received, shift_by):
    rolled = jnp.roll(received, -shift_by, axis=0)
    return jnp.swapaxes(rolled, 0, 1).reshape(-1, received.shape[2])


def from_request(request_rows, shift_by, source_count):
    shaped = request_rows.reshape(-1, source_count, request_rows.shape[1])
    return jnp.roll(jnp.swapaxes(shaped, 0, 1), shift_by, axis=0)


def ring_gather(narrow, axis_name):
    count = lax.axis_size(axis_name)
    position = lax.axis_index(axis_name)
    stacked = [narrow]
    for shift in range(1, count):
        perm = [(index, (index - shift) % count) for index in range(count)]
        stacked.append(lax.ppermute(narrow, axis_name, perm))
    ordered = jnp.roll(jnp.stack(stacked, axis=0), position, axis=0)
    return jnp.concatenate([ordered[index] for index in range(count)], axis=1)


def ring_reduce_scatter(partial_rows, axis_name):
    count = lax.axis_size(axis_name)
    position = lax.axis_index(axis_name)
    width = partial_rows.shape[1] // count
    blocks = partial_rows.astype(jnp.bfloat16).reshape(partial_rows.shape[0], count, width)
    total = lax.dynamic_index_in_dim(blocks, position, 1, keepdims=False).astype(jnp.float32)
    for shift in range(1, count):
        perm = [(index, (index + shift) % count) for index in range(count)]
        outgoing = lax.dynamic_index_in_dim(blocks, (position + shift) % count, 1, keepdims=False)
        total = total + lax.ppermute(outgoing, axis_name, perm).astype(jnp.float32)
    return total.astype(jnp.bfloat16)


def body(
    hidden_in,
    norm_gain,
    query_weight,
    keyval_weight,
    output_weight,
    segment_ids,
    request_lengths,
    request_owner,
    cache_slots,
):
    source_count = lax.axis_size("seq")
    source_pos = lax.axis_index("seq")
    local_rows = hidden_in.shape[0]
    capacity = MAXLEN // source_count
    chunk_slots = capacity // CHUNKS
    chunk_rows = chunk_slots * source_count
    request_ids = jnp.arange(source_count, dtype=jnp.int32)
    starts = jnp.cumsum(request_lengths) - request_lengths
    first_row = jnp.maximum((starts - source_pos + source_count - 1) // source_count, 0)
    owner_match = request_owner[None, :] == request_ids[:, None]
    owned_by = jnp.sum(jnp.where(owner_match, request_ids[None, :], 0), axis=1)
    send_first = jnp.sum(jnp.where(owner_match, first_row[None, :], 0), axis=1)
    row_index = send_first[:, None] + jnp.arange(capacity, dtype=jnp.int32)[None, :]
    safe_index = jnp.minimum(row_index, local_rows - 1)
    live_send = (row_index < local_rows) & (segment_ids[safe_index] == owned_by[:, None])
    owned_request = jnp.sum(jnp.where(request_owner == source_pos, request_ids, 0))
    own_match = request_ids == owned_request
    own_start = jnp.sum(jnp.where(own_match, starts, 0))
    own_length = jnp.sum(jnp.where(own_match, request_lengths, 0))
    own_slot = jnp.sum(jnp.where(own_match, cache_slots, 0))
    shift_by = own_start % source_count
    picked = jnp.where(live_send[:, :, None], hidden_in[safe_index], jnp.zeros((), jnp.bfloat16))
    head_count = query_weight.shape[1] // HD
    per_group = HEADS // KV_HEADS
    block_count = keyval_weight.shape[1] // HD
    key_chunks = []
    value_chunks = []
    cached_chunks = []
    returned_chunks = []
    for chunk in range(CHUNKS):
        chunk_first = chunk * chunk_rows
        arrived = lax.all_to_all(
            picked[:, chunk * chunk_slots : (chunk + 1) * chunk_slots],
            "seq",
            split_axis=0,
            concat_axis=0,
            tiled=True,
        )
        narrow_rows = to_request(arrived, shift_by)
        full_rows = ring_gather(narrow_rows, "tensor")
        normed = normalize(full_rows, norm_gain)
        queries = jnp.dot(normed, query_weight, preferred_element_type=jnp.float32)
        keyvals = jnp.dot(normed, keyval_weight, preferred_element_type=jnp.float32)
        rotated_query = rotate_rows(queries, HD, chunk_first).astype(jnp.bfloat16)
        own_blocks = []
        for block_index in range(block_count):
            plain_block = keyvals[:, block_index * HD : (block_index + 1) * HD]
            if block_index % 2 == 0:
                own_blocks.append(rotate_rows(plain_block, HD, chunk_first).astype(jnp.bfloat16))
            else:
                own_blocks.append(plain_block.astype(jnp.bfloat16))
        own_cached = jnp.concatenate(own_blocks, axis=1)
        cached_chunks.append(own_cached)
        key_chunks.append(own_cached[:, 0:HD])
        value_chunks.append(own_cached[:, HD : 2 * HD])
        key_rows = jnp.concatenate(key_chunks, axis=0)
        value_rows = jnp.concatenate(value_chunks, axis=0)
        head_outputs = []
        for head_index in range(head_count):
            head_outputs.append(
                attend(
                    rotated_query[:, head_index * HD : (head_index + 1) * HD],
                    chunk_first,
                    key_rows,
                    value_rows,
                    own_length,
                )
            )
        attention_rows = jnp.concatenate(head_outputs, axis=1)
        outgoing = from_request(attention_rows, shift_by, source_count)
        returned_chunks.append(
            lax.all_to_all(outgoing, "seq", split_axis=0, concat_axis=0, tiled=True)
        )
    returned = jnp.concatenate(returned_chunks, axis=1)
    segment_match = segment_ids[:, None] == request_ids[None, :]
    row_owner = jnp.sum(jnp.where(segment_match, request_owner[None, :], 0), axis=1)
    row_first = jnp.sum(jnp.where(segment_match, first_row[None, :], 0), axis=1)
    slot_pos = jnp.arange(local_rows, dtype=jnp.int32) - row_first
    usable = (segment_ids >= 0) & (slot_pos >= 0) & (slot_pos < capacity)
    flat_index = row_owner * capacity + jnp.clip(slot_pos, 0, capacity - 1)
    flattened = returned.reshape(-1, returned.shape[2])
    local_attention = jnp.where(usable[:, None], flattened[flat_index], jnp.zeros((), returned.dtype))
    partial_sum = jnp.dot(local_attention, output_weight, preferred_element_type=jnp.float32)
    attended = ring_reduce_scatter(partial_sum, "tensor")
    all_cached = jnp.concatenate(cached_chunks, axis=0)
    slot_ids = jnp.arange(SLOTS_DEV, dtype=jnp.int32)
    cache_table = jnp.where(
        (slot_ids == own_slot)[:, None, None], all_cached[None], jnp.zeros((), jnp.bfloat16)
    )
    return (attended, cache_table)


def solution(mesh):
    in_specs = (
        P("seq", "tensor"),
        P(),
        P(None, "tensor"),
        P(None, "tensor"),
        P("tensor", None),
        P("seq"),
        P(),
        P(),
        P(),
    )
    out_specs = (P("seq", "tensor"), P("seq", None, "tensor"))
    return jax.shard_map(body, mesh=mesh, in_specs=in_specs, out_specs=out_specs, check_vma=False)
```

```python
import jax
import jax.numpy as jnp
from jax import lax
from jax.sharding import PartitionSpec as P

HEADS = 8
KV_HEADS = 4
HD = 256
SLOTS_DEV = 2
MAXLEN = 512


EPSILON = 1e-06
ROPE_BASE = 1000042.0
CHUNKS = 1


def rotate_rows(values, head_size, first_pos):
    row_count = values.shape[0]
    shaped = values.reshape(row_count, -1, head_size)
    half_size = head_size // 2
    frequency = ROPE_BASE ** (jnp.arange(half_size, dtype=jnp.float32) * (-2.0 / head_size))
    positions = (first_pos + jnp.arange(row_count, dtype=jnp.int32)).astype(jnp.float32)
    angles = positions[:, None] * frequency[None, :]
    cosine_table = jnp.cos(angles)[:, None, :]
    sine_table = jnp.sin(angles)[:, None, :]
    first_half = shaped[..., :half_size]
    second_half = shaped[..., half_size:]
    turned = jnp.concatenate(
        [
            first_half * cosine_table - second_half * sine_table,
            second_half * cosine_table + first_half * sine_table,
        ],
        axis=-1,
    )
    return turned.reshape(values.shape)


def normalize(rows_in, gain):
    widened = rows_in.astype(jnp.float32)
    inverse_rms = lax.rsqrt(jnp.mean(widened * widened, axis=-1, keepdims=True) + EPSILON)
    return (widened * inverse_rms * gain.astype(jnp.float32)).astype(jnp.bfloat16)


def attend(query_block, start_row, key_rows, value_rows, length):
    row_count = query_block.shape[0]
    scores = jnp.dot(query_block, key_rows.T, preferred_element_type=jnp.float32) * key_rows.shape[
        1
    ] ** (-0.5)
    query_pos = start_row + jnp.arange(row_count, dtype=jnp.int32)[:, None]
    key_pos = jnp.arange(key_rows.shape[0], dtype=jnp.int32)[None, :]
    allowed = (key_pos <= query_pos) & (key_pos < length)
    scores = jnp.where(allowed, scores, -jnp.inf)
    row_top = jnp.max(scores, axis=-1, keepdims=True)
    powered = jnp.exp(scores - row_top)
    weights = (powered / jnp.sum(powered, axis=-1, keepdims=True)).astype(jnp.bfloat16)
    return jnp.dot(weights, value_rows, preferred_element_type=jnp.float32).astype(jnp.bfloat16)


def to_request(received, shift_by):
    rolled = jnp.roll(received, -shift_by, axis=0)
    return jnp.swapaxes(rolled, 0, 1).reshape(-1, received.shape[2])


def from_request(request_rows, shift_by, source_count):
    shaped = request_rows.reshape(-1, source_count, request_rows.shape[1])
    return jnp.roll(jnp.swapaxes(shaped, 0, 1), shift_by, axis=0)


def ring_blocks(narrow, axis_name):
    count = lax.axis_size(axis_name)
    blocks = [narrow]
    for shift in range(1, count):
        perm = [(index, (index - shift) % count) for index in range(count)]
        blocks.append(lax.ppermute(narrow, axis_name, perm))
    return blocks


def project_blocks(blocks, gain, query_weight, keyval_weight, axis_name):
    count = lax.axis_size(axis_name)
    position = lax.axis_index(axis_name)
    width = blocks[0].shape[1]
    widened = [block.astype(jnp.float32) for block in blocks]
    squares = sum(jnp.sum(block * block, axis=-1, keepdims=True) for block in widened)
    inverse_rms = lax.rsqrt(squares / (width * count) + EPSILON)
    queries = None
    keyvals = None
    for shift, block in enumerate(widened):
        first = ((position + shift) % count) * width
        block_gain = lax.dynamic_slice_in_dim(gain, first, width, 0).astype(jnp.float32)
        normed = (block * inverse_rms * block_gain).astype(jnp.bfloat16)
        query_part = jnp.dot(
            normed,
            lax.dynamic_slice_in_dim(query_weight, first, width, 0),
            preferred_element_type=jnp.float32,
        )
        keyval_part = jnp.dot(
            normed,
            lax.dynamic_slice_in_dim(keyval_weight, first, width, 0),
            preferred_element_type=jnp.float32,
        )
        queries = query_part if queries is None else queries + query_part
        keyvals = keyval_part if keyvals is None else keyvals + keyval_part
    return queries, keyvals


def ring_output(local_attention, output_weight, axis_name):
    count = lax.axis_size(axis_name)
    position = lax.axis_index(axis_name)
    width = output_weight.shape[1] // count
    total = None
    for shift in range(count):
        first = ((position + shift) % count) * width
        part = jnp.dot(
            local_attention,
            lax.dynamic_slice_in_dim(output_weight, first, width, 1),
            preferred_element_type=jnp.float32,
        ).astype(jnp.bfloat16)
        if shift == 0:
            total = part.astype(jnp.float32)
        else:
            perm = [(index, (index + shift) % count) for index in range(count)]
            total = total + lax.ppermute(part, axis_name, perm).astype(jnp.float32)
    return total.astype(jnp.bfloat16)


def body(
    hidden_in,
    norm_gain,
    query_weight,
    keyval_weight,
    output_weight,
    segment_ids,
    request_lengths,
    request_owner,
    cache_slots,
):
    source_count = lax.axis_size("seq")
    source_pos = lax.axis_index("seq")
    local_rows = hidden_in.shape[0]
    capacity = MAXLEN // source_count
    chunk_slots = capacity // CHUNKS
    chunk_rows = chunk_slots * source_count
    request_ids = jnp.arange(source_count, dtype=jnp.int32)
    starts = jnp.cumsum(request_lengths) - request_lengths
    first_row = jnp.maximum((starts - source_pos + source_count - 1) // source_count, 0)
    owner_match = request_owner[None, :] == request_ids[:, None]
    send_first = jnp.sum(jnp.where(owner_match, first_row[None, :], 0), axis=1)
    send_start = jnp.sum(jnp.where(owner_match, starts[None, :], 0), axis=1)
    send_length = jnp.sum(jnp.where(owner_match, request_lengths[None, :], 0), axis=1)
    row_index = send_first[:, None] + jnp.arange(capacity, dtype=jnp.int32)[None, :]
    stream_pos = row_index * source_count + source_pos
    live_send = (
        (row_index < local_rows)
        & (stream_pos >= send_start[:, None])
        & (stream_pos < (send_start + send_length)[:, None])
    )
    local_ids = jnp.arange(local_rows, dtype=jnp.int32)
    select = (
        (row_index.reshape(-1)[:, None] == local_ids[None, :]) & live_send.reshape(-1)[:, None]
    ).astype(jnp.bfloat16)
    owned_request = jnp.sum(jnp.where(request_owner == source_pos, request_ids, 0))
    own_match = request_ids == owned_request
    own_start = jnp.sum(jnp.where(own_match, starts, 0))
    own_length = jnp.sum(jnp.where(own_match, request_lengths, 0))
    own_slot = jnp.sum(jnp.where(own_match, cache_slots, 0))
    shift_by = own_start % source_count
    picked = (
        jnp.dot(select, hidden_in, preferred_element_type=jnp.float32)
        .astype(jnp.bfloat16)
        .reshape(source_count, capacity, hidden_in.shape[1])
    )
    head_count = query_weight.shape[1] // HD
    per_group = HEADS // KV_HEADS
    block_count = keyval_weight.shape[1] // HD
    key_chunks = []
    value_chunks = []
    cached_chunks = []
    returned_chunks = []
    for chunk in range(CHUNKS):
        chunk_first = chunk * chunk_rows
        arrived = lax.all_to_all(
            picked[:, chunk * chunk_slots : (chunk + 1) * chunk_slots],
            "seq",
            split_axis=0,
            concat_axis=0,
            tiled=True,
        )
        narrow_rows = to_request(arrived, shift_by)
        queries, keyvals = project_blocks(
            ring_blocks(narrow_rows, "tensor"), norm_gain, query_weight, keyval_weight, "tensor"
        )
        rotated_query = rotate_rows(queries, HD, chunk_first).astype(jnp.bfloat16)
        own_blocks = []
        for block_index in range(block_count):
            plain_block = keyvals[:, block_index * HD : (block_index + 1) * HD]
            if block_index % 2 == 0:
                own_blocks.append(rotate_rows(plain_block, HD, chunk_first).astype(jnp.bfloat16))
            else:
                own_blocks.append(plain_block.astype(jnp.bfloat16))
        own_cached = jnp.concatenate(own_blocks, axis=1)
        cached_chunks.append(own_cached)
        key_chunks.append(own_cached[:, 0:HD])
        value_chunks.append(own_cached[:, HD : 2 * HD])
        key_rows = jnp.concatenate(key_chunks, axis=0)
        value_rows = jnp.concatenate(value_chunks, axis=0)
        head_outputs = []
        for head_index in range(head_count):
            head_outputs.append(
                attend(
                    rotated_query[:, head_index * HD : (head_index + 1) * HD],
                    chunk_first,
                    key_rows,
                    value_rows,
                    own_length,
                )
            )
        attention_rows = jnp.concatenate(head_outputs, axis=1)
        outgoing = from_request(attention_rows, shift_by, source_count)
        returned_chunks.append(
            lax.all_to_all(outgoing, "seq", split_axis=0, concat_axis=0, tiled=True)
        )
    returned = jnp.concatenate(returned_chunks, axis=1)
    flattened = returned.reshape(-1, returned.shape[2])
    local_attention = lax.dot_general(
        select, flattened, (((0,), (0,)), ((), ())), preferred_element_type=jnp.float32
    ).astype(jnp.bfloat16)
    attended = ring_output(local_attention, output_weight, "tensor")
    all_cached = jnp.concatenate(cached_chunks, axis=0)
    slot_ids = jnp.arange(SLOTS_DEV, dtype=jnp.int32)
    cache_table = jnp.where(
        (slot_ids == own_slot)[:, None, None], all_cached[None], jnp.zeros((), jnp.bfloat16)
    )
    return (attended, cache_table)


def solution(mesh):
    in_specs = (
        P("seq", "tensor"),
        P(),
        P(None, "tensor"),
        P(None, "tensor"),
        P("tensor", None),
        P("seq"),
        P(),
        P(),
        P(),
    )
    out_specs = (P("seq", "tensor"), P("seq", None, "tensor"))
    return jax.shard_map(body, mesh=mesh, in_specs=in_specs, out_specs=out_specs, check_vma=False)
```

```python
import jax
import jax.numpy as jnp
from jax import lax
from jax.sharding import PartitionSpec as P

HEADS = 8
KV_HEADS = 4
HD = 256
SLOTS_DEV = 2
MAXLEN = 512


EPSILON = 1e-06
ROPE_BASE = 1000042.0
CHUNKS = 1


def rotate_rows(values, head_size, row_pos):
    row_count = values.shape[0]
    shaped = values.reshape(row_count, -1, head_size)
    half_size = head_size // 2
    frequency = ROPE_BASE ** (jnp.arange(half_size, dtype=jnp.float32) * (-2.0 / head_size))
    positions = row_pos.astype(jnp.float32)
    angles = positions[:, None] * frequency[None, :]
    cosine_table = jnp.cos(angles)[:, None, :]
    sine_table = jnp.sin(angles)[:, None, :]
    first_half = shaped[..., :half_size]
    second_half = shaped[..., half_size:]
    turned = jnp.concatenate(
        [
            first_half * cosine_table - second_half * sine_table,
            second_half * cosine_table + first_half * sine_table,
        ],
        axis=-1,
    )
    return turned.reshape(values.shape)


def normalize(rows_in, gain):
    widened = rows_in.astype(jnp.float32)
    inverse_rms = lax.rsqrt(jnp.mean(widened * widened, axis=-1, keepdims=True) + EPSILON)
    return (widened * inverse_rms * gain.astype(jnp.float32)).astype(jnp.bfloat16)


def attend(query_block, query_pos, key_rows, key_pos, value_rows, length):
    scores = jnp.dot(query_block, key_rows.T, preferred_element_type=jnp.float32) * key_rows.shape[
        1
    ] ** (-0.5)
    allowed = (key_pos[None, :] <= query_pos[:, None]) & (key_pos[None, :] < length)
    scores = jnp.where(allowed, scores, -jnp.inf)
    row_top = jnp.max(scores, axis=-1, keepdims=True)
    powered = jnp.exp(scores - row_top)
    weights = (powered / jnp.sum(powered, axis=-1, keepdims=True)).astype(jnp.bfloat16)
    return jnp.dot(weights, value_rows, preferred_element_type=jnp.float32).astype(jnp.bfloat16)


def to_request(received, shift_by):
    rolled = jnp.roll(received, -shift_by, axis=0)
    return jnp.swapaxes(rolled, 0, 1).reshape(-1, received.shape[2])


def from_request(request_rows, shift_by, source_count):
    shaped = request_rows.reshape(-1, source_count, request_rows.shape[1])
    return jnp.roll(jnp.swapaxes(shaped, 0, 1), shift_by, axis=0)


def ring_blocks(narrow, axis_name):
    count = lax.axis_size(axis_name)
    blocks = [narrow]
    for shift in range(1, count):
        perm = [(index, (index - shift) % count) for index in range(count)]
        blocks.append(lax.ppermute(narrow, axis_name, perm))
    return blocks


def project_blocks(blocks, gain, query_weight, keyval_weight, axis_name):
    count = lax.axis_size(axis_name)
    position = lax.axis_index(axis_name)
    width = blocks[0].shape[1]
    widened = [block.astype(jnp.float32) for block in blocks]
    squares = sum(jnp.sum(block * block, axis=-1, keepdims=True) for block in widened)
    inverse_rms = lax.rsqrt(squares / (width * count) + EPSILON)
    queries = None
    keyvals = None
    for shift, block in enumerate(widened):
        first = ((position + shift) % count) * width
        block_gain = lax.dynamic_slice_in_dim(gain, first, width, 0).astype(jnp.float32)
        normed = (block * inverse_rms * block_gain).astype(jnp.bfloat16)
        query_part = jnp.dot(
            normed,
            lax.dynamic_slice_in_dim(query_weight, first, width, 0),
            preferred_element_type=jnp.float32,
        )
        keyval_part = jnp.dot(
            normed,
            lax.dynamic_slice_in_dim(keyval_weight, first, width, 0),
            preferred_element_type=jnp.float32,
        )
        queries = query_part if queries is None else queries + query_part
        keyvals = keyval_part if keyvals is None else keyvals + keyval_part
    return queries, keyvals


def ring_output(local_attention, output_weight, axis_name):
    count = lax.axis_size(axis_name)
    position = lax.axis_index(axis_name)
    width = output_weight.shape[1] // count
    total = None
    for shift in range(count):
        first = ((position + shift) % count) * width
        part = jnp.dot(
            local_attention,
            lax.dynamic_slice_in_dim(output_weight, first, width, 1),
            preferred_element_type=jnp.float32,
        ).astype(jnp.bfloat16)
        if shift == 0:
            total = part.astype(jnp.float32)
        else:
            perm = [(index, (index + shift) % count) for index in range(count)]
            total = total + lax.ppermute(part, axis_name, perm).astype(jnp.float32)
    return total.astype(jnp.bfloat16)


def body(
    hidden_in,
    norm_gain,
    query_weight,
    keyval_weight,
    output_weight,
    segment_ids,
    request_lengths,
    request_owner,
    cache_slots,
):
    source_count = lax.axis_size("seq")
    source_pos = lax.axis_index("seq")
    local_rows = hidden_in.shape[0]
    capacity = MAXLEN // source_count
    chunk_slots = capacity // CHUNKS
    chunk_rows = chunk_slots * source_count
    request_ids = jnp.arange(source_count, dtype=jnp.int32)
    starts = jnp.cumsum(request_lengths) - request_lengths
    first_row = jnp.maximum((starts - source_pos + source_count - 1) // source_count, 0)
    owner_match = request_owner[None, :] == request_ids[:, None]
    send_first = jnp.sum(jnp.where(owner_match, first_row[None, :], 0), axis=1)
    send_start = jnp.sum(jnp.where(owner_match, starts[None, :], 0), axis=1)
    send_length = jnp.sum(jnp.where(owner_match, request_lengths[None, :], 0), axis=1)
    row_index = send_first[:, None] + jnp.arange(capacity, dtype=jnp.int32)[None, :]
    stream_pos = row_index * source_count + source_pos
    live_send = (
        (row_index < local_rows)
        & (stream_pos >= send_start[:, None])
        & (stream_pos < (send_start + send_length)[:, None])
    )
    local_ids = jnp.arange(local_rows, dtype=jnp.int32)
    select = (
        (row_index.T.reshape(-1)[:, None] == local_ids[None, :]) & live_send.T.reshape(-1)[:, None]
    ).astype(jnp.bfloat16)
    owned_request = jnp.sum(jnp.where(request_owner == source_pos, request_ids, 0))
    own_match = request_ids == owned_request
    own_start = jnp.sum(jnp.where(own_match, starts, 0))
    own_length = jnp.sum(jnp.where(own_match, request_lengths, 0))
    own_slot = jnp.sum(jnp.where(own_match, cache_slots, 0))
    shift_by = own_start % source_count
    picked = (
        jnp.dot(select, hidden_in, preferred_element_type=jnp.float32)
        .astype(jnp.bfloat16)
        .reshape(capacity, source_count, hidden_in.shape[1])
    )
    source_ids = jnp.arange(source_count, dtype=jnp.int32)
    slot_ids_all = jnp.arange(capacity, dtype=jnp.int32)
    row_pos = (
        slot_ids_all[:, None] * source_count + (source_ids[None, :] - shift_by) % source_count
    ).reshape(-1)
    head_count = query_weight.shape[1] // HD
    per_group = HEADS // KV_HEADS
    block_count = keyval_weight.shape[1] // HD
    key_chunks = []
    value_chunks = []
    cached_chunks = []
    returned_chunks = []
    for chunk in range(CHUNKS):
        chunk_first = chunk * chunk_rows
        arrived = lax.all_to_all(
            picked[chunk * chunk_slots : (chunk + 1) * chunk_slots],
            "seq",
            split_axis=1,
            concat_axis=1,
            tiled=True,
        )
        narrow_rows = arrived.reshape(-1, arrived.shape[2])
        chunk_pos = row_pos[chunk * chunk_rows : (chunk + 1) * chunk_rows]
        queries, keyvals = project_blocks(
            ring_blocks(narrow_rows, "tensor"), norm_gain, query_weight, keyval_weight, "tensor"
        )
        rotated_query = rotate_rows(queries, HD, chunk_pos).astype(jnp.bfloat16)
        own_blocks = []
        for block_index in range(block_count):
            plain_block = keyvals[:, block_index * HD : (block_index + 1) * HD]
            if block_index % 2 == 0:
                own_blocks.append(rotate_rows(plain_block, HD, chunk_pos).astype(jnp.bfloat16))
            else:
                own_blocks.append(plain_block.astype(jnp.bfloat16))
        own_cached = jnp.concatenate(own_blocks, axis=1)
        cached_chunks.append(own_cached)
        key_chunks.append(own_cached[:, 0:HD])
        value_chunks.append(own_cached[:, HD : 2 * HD])
        key_rows = jnp.concatenate(key_chunks, axis=0)
        value_rows = jnp.concatenate(value_chunks, axis=0)
        head_outputs = []
        for head_index in range(head_count):
            head_outputs.append(
                attend(
                    rotated_query[:, head_index * HD : (head_index + 1) * HD],
                    chunk_pos,
                    key_rows,
                    row_pos[: (chunk + 1) * chunk_rows],
                    value_rows,
                    own_length,
                )
            )
        attention_rows = jnp.concatenate(head_outputs, axis=1)
        outgoing = attention_rows.reshape(chunk_slots, source_count, attention_rows.shape[1])
        returned_chunks.append(
            lax.all_to_all(outgoing, "seq", split_axis=1, concat_axis=1, tiled=True)
        )
    returned = jnp.concatenate(returned_chunks, axis=0)
    flattened = returned.reshape(-1, returned.shape[2])
    local_attention = lax.dot_general(
        select, flattened, (((0,), (0,)), ((), ())), preferred_element_type=jnp.float32
    ).astype(jnp.bfloat16)
    attended = ring_output(local_attention, output_weight, "tensor")
    all_cached = to_request(
        jnp.swapaxes(jnp.concatenate(cached_chunks, axis=0).reshape(capacity, source_count, -1), 0, 1),
        shift_by,
    )
    slot_ids = jnp.arange(SLOTS_DEV, dtype=jnp.int32)
    cache_table = jnp.where(
        (slot_ids == own_slot)[:, None, None], all_cached[None], jnp.zeros((), jnp.bfloat16)
    )
    return (attended, cache_table)


def solution(mesh):
    in_specs = (
        P("seq", "tensor"),
        P(),
        P(None, "tensor"),
        P(None, "tensor"),
        P("tensor", None),
        P("seq"),
        P(),
        P(),
        P(),
    )
    out_specs = (P("seq", "tensor"), P("seq", None, "tensor"))
    return jax.shard_map(body, mesh=mesh, in_specs=in_specs, out_specs=out_specs, check_vma=False)
```

```python
import jax
import jax.numpy as jnp
from jax import lax
from jax.sharding import PartitionSpec as P

HEADS = 8
KV_HEADS = 4
HD = 256
SLOTS_DEV = 2
MAXLEN = 512


EPSILON = 1e-06
ROPE_BASE = 1000042.0
CHUNKS = 1


def rotate_rows(values, head_size, first_pos):
    row_count = values.shape[0]
    shaped = values.reshape(row_count, -1, head_size)
    half_size = head_size // 2
    frequency = ROPE_BASE ** (jnp.arange(half_size, dtype=jnp.float32) * (-2.0 / head_size))
    positions = (first_pos + jnp.arange(row_count, dtype=jnp.int32)).astype(jnp.float32)
    angles = positions[:, None] * frequency[None, :]
    cosine_table = jnp.cos(angles)[:, None, :]
    sine_table = jnp.sin(angles)[:, None, :]
    first_half = shaped[..., :half_size]
    second_half = shaped[..., half_size:]
    turned = jnp.concatenate(
        [
            first_half * cosine_table - second_half * sine_table,
            second_half * cosine_table + first_half * sine_table,
        ],
        axis=-1,
    )
    return turned.reshape(values.shape)


def normalize(rows_in, gain):
    widened = rows_in.astype(jnp.float32)
    inverse_rms = lax.rsqrt(jnp.mean(widened * widened, axis=-1, keepdims=True) + EPSILON)
    return (widened * inverse_rms * gain.astype(jnp.float32)).astype(jnp.bfloat16)


def attend(query_block, start_row, key_rows, value_rows, length):
    row_count = query_block.shape[0]
    scores = jnp.dot(query_block, key_rows.T, preferred_element_type=jnp.float32) * key_rows.shape[
        1
    ] ** (-0.5)
    query_pos = start_row + jnp.arange(row_count, dtype=jnp.int32)[:, None]
    key_pos = jnp.arange(key_rows.shape[0], dtype=jnp.int32)[None, :]
    allowed = (key_pos <= query_pos) & (key_pos < length)
    scores = jnp.where(allowed, scores, -jnp.inf)
    row_top = jnp.max(scores, axis=-1, keepdims=True)
    powered = jnp.exp(scores - row_top)
    weights = (powered / jnp.sum(powered, axis=-1, keepdims=True)).astype(jnp.bfloat16)
    return jnp.dot(weights, value_rows, preferred_element_type=jnp.float32).astype(jnp.bfloat16)


def to_request(received, shift_by):
    rolled = jnp.roll(received, -shift_by, axis=0)
    return jnp.swapaxes(rolled, 0, 1).reshape(-1, received.shape[2])


def from_request(request_rows, shift_by, source_count):
    shaped = request_rows.reshape(-1, source_count, request_rows.shape[1])
    return jnp.roll(jnp.swapaxes(shaped, 0, 1), shift_by, axis=0)


def ring_blocks(narrow, axis_name):
    count = lax.axis_size(axis_name)
    to_left = [(index, (index - 1) % count) for index in range(count)]
    to_right = [(index, (index + 1) % count) for index in range(count)]
    from_right = lax.ppermute(narrow, axis_name, to_left)
    from_left = lax.ppermute(narrow, axis_name, to_right)
    if count != 4:
        blocks = [narrow]
        for shift in range(1, count):
            perm = [(index, (index - shift) % count) for index in range(count)]
            blocks.append(lax.ppermute(narrow, axis_name, perm))
        return blocks
    half = narrow.shape[1] // 2
    across = jnp.concatenate(
        [
            lax.ppermute(from_right[:, :half], axis_name, to_left),
            lax.ppermute(from_left[:, half:], axis_name, to_right),
        ],
        axis=1,
    )
    return [narrow, from_right, across, from_left]


def project_blocks(blocks, gain, query_weight, keyval_weight, axis_name):
    count = lax.axis_size(axis_name)
    position = lax.axis_index(axis_name)
    width = blocks[0].shape[1]
    widened = [block.astype(jnp.float32) for block in blocks]
    squares = sum(jnp.sum(block * block, axis=-1, keepdims=True) for block in widened)
    inverse_rms = lax.rsqrt(squares / (width * count) + EPSILON)
    queries = None
    keyvals = None
    for shift, block in enumerate(widened):
        first = ((position + shift) % count) * width
        block_gain = lax.dynamic_slice_in_dim(gain, first, width, 0).astype(jnp.float32)
        normed = (block * inverse_rms * block_gain).astype(jnp.bfloat16)
        query_part = jnp.dot(
            normed,
            lax.dynamic_slice_in_dim(query_weight, first, width, 0),
            preferred_element_type=jnp.float32,
        )
        keyval_part = jnp.dot(
            normed,
            lax.dynamic_slice_in_dim(keyval_weight, first, width, 0),
            preferred_element_type=jnp.float32,
        )
        queries = query_part if queries is None else queries + query_part
        keyvals = keyval_part if keyvals is None else keyvals + keyval_part
    return queries, keyvals


def ring_output(local_attention, output_weight, axis_name):
    count = lax.axis_size(axis_name)
    position = lax.axis_index(axis_name)
    width = output_weight.shape[1] // count
    total = None
    for shift in range(count):
        first = ((position + shift) % count) * width
        part = jnp.dot(
            local_attention,
            lax.dynamic_slice_in_dim(output_weight, first, width, 1),
            preferred_element_type=jnp.float32,
        ).astype(jnp.bfloat16)
        if shift == 0:
            total = part.astype(jnp.float32)
        else:
            perm = [(index, (index + shift) % count) for index in range(count)]
            total = total + lax.ppermute(part, axis_name, perm).astype(jnp.float32)
    return total.astype(jnp.bfloat16)


def body(
    hidden_in,
    norm_gain,
    query_weight,
    keyval_weight,
    output_weight,
    segment_ids,
    request_lengths,
    request_owner,
    cache_slots,
):
    source_count = lax.axis_size("seq")
    source_pos = lax.axis_index("seq")
    local_rows = hidden_in.shape[0]
    capacity = MAXLEN // source_count
    chunk_slots = capacity // CHUNKS
    chunk_rows = chunk_slots * source_count
    request_ids = jnp.arange(source_count, dtype=jnp.int32)
    starts = jnp.cumsum(request_lengths) - request_lengths
    first_row = jnp.maximum((starts - source_pos + source_count - 1) // source_count, 0)
    owner_match = request_owner[None, :] == request_ids[:, None]
    send_first = jnp.sum(jnp.where(owner_match, first_row[None, :], 0), axis=1)
    send_start = jnp.sum(jnp.where(owner_match, starts[None, :], 0), axis=1)
    send_length = jnp.sum(jnp.where(owner_match, request_lengths[None, :], 0), axis=1)
    row_index = send_first[:, None] + jnp.arange(capacity, dtype=jnp.int32)[None, :]
    stream_pos = row_index * source_count + source_pos
    live_send = (
        (row_index < local_rows)
        & (stream_pos >= send_start[:, None])
        & (stream_pos < (send_start + send_length)[:, None])
    )
    local_ids = jnp.arange(local_rows, dtype=jnp.int32)
    select = (
        (row_index.reshape(-1)[:, None] == local_ids[None, :]) & live_send.reshape(-1)[:, None]
    ).astype(jnp.bfloat16)
    owned_request = jnp.sum(jnp.where(request_owner == source_pos, request_ids, 0))
    own_match = request_ids == owned_request
    own_start = jnp.sum(jnp.where(own_match, starts, 0))
    own_length = jnp.sum(jnp.where(own_match, request_lengths, 0))
    own_slot = jnp.sum(jnp.where(own_match, cache_slots, 0))
    shift_by = own_start % source_count
    picked = (
        jnp.dot(select, hidden_in, preferred_element_type=jnp.float32)
        .astype(jnp.bfloat16)
        .reshape(source_count, capacity, hidden_in.shape[1])
    )
    head_count = query_weight.shape[1] // HD
    per_group = HEADS // KV_HEADS
    block_count = keyval_weight.shape[1] // HD
    key_chunks = []
    value_chunks = []
    cached_chunks = []
    returned_chunks = []
    for chunk in range(CHUNKS):
        chunk_first = chunk * chunk_rows
        arrived = lax.all_to_all(
            picked[:, chunk * chunk_slots : (chunk + 1) * chunk_slots],
            "seq",
            split_axis=0,
            concat_axis=0,
            tiled=True,
        )
        narrow_rows = to_request(arrived, shift_by)
        queries, keyvals = project_blocks(
            ring_blocks(narrow_rows, "tensor"), norm_gain, query_weight, keyval_weight, "tensor"
        )
        rotated_query = rotate_rows(queries, HD, chunk_first).astype(jnp.bfloat16)
        own_blocks = []
        for block_index in range(block_count):
            plain_block = keyvals[:, block_index * HD : (block_index + 1) * HD]
            if block_index % 2 == 0:
                own_blocks.append(rotate_rows(plain_block, HD, chunk_first).astype(jnp.bfloat16))
            else:
                own_blocks.append(plain_block.astype(jnp.bfloat16))
        own_cached = jnp.concatenate(own_blocks, axis=1)
        cached_chunks.append(own_cached)
        key_chunks.append(own_cached[:, 0:HD])
        value_chunks.append(own_cached[:, HD : 2 * HD])
        key_rows = jnp.concatenate(key_chunks, axis=0)
        value_rows = jnp.concatenate(value_chunks, axis=0)
        head_outputs = []
        for head_index in range(head_count):
            head_outputs.append(
                attend(
                    rotated_query[:, head_index * HD : (head_index + 1) * HD],
                    chunk_first,
                    key_rows,
                    value_rows,
                    own_length,
                )
            )
        attention_rows = jnp.concatenate(head_outputs, axis=1)
        outgoing = from_request(attention_rows, shift_by, source_count)
        returned_chunks.append(
            lax.all_to_all(outgoing, "seq", split_axis=0, concat_axis=0, tiled=True)
        )
    returned = jnp.concatenate(returned_chunks, axis=1)
    flattened = returned.reshape(-1, returned.shape[2])
    local_attention = lax.dot_general(
        select, flattened, (((0,), (0,)), ((), ())), preferred_element_type=jnp.float32
    ).astype(jnp.bfloat16)
    attended = ring_output(local_attention, output_weight, "tensor")
    all_cached = jnp.concatenate(cached_chunks, axis=0)
    slot_ids = jnp.arange(SLOTS_DEV, dtype=jnp.int32)
    cache_table = jnp.where(
        (slot_ids == own_slot)[:, None, None], all_cached[None], jnp.zeros((), jnp.bfloat16)
    )
    return (attended, cache_table)


def solution(mesh):
    in_specs = (
        P("seq", "tensor"),
        P(),
        P(None, "tensor"),
        P(None, "tensor"),
        P("tensor", None),
        P("seq"),
        P(),
        P(),
        P(),
    )
    out_specs = (P("seq", "tensor"), P("seq", None, "tensor"))
    return jax.shard_map(body, mesh=mesh, in_specs=in_specs, out_specs=out_specs, check_vma=False)
```

```python
import jax
import jax.numpy as jnp
from jax import lax
from jax.sharding import PartitionSpec as P

HEADS = 8
KV_HEADS = 4
HD = 256
SLOTS_DEV = 2
MAXLEN = 512


EPSILON = 1e-06
ROPE_BASE = 1000042.0
CHUNKS = 1


def rotate_rows(values, head_size, first_pos):
    row_count = values.shape[0]
    shaped = values.reshape(row_count, -1, head_size)
    half_size = head_size // 2
    frequency = ROPE_BASE ** (jnp.arange(half_size, dtype=jnp.float32) * (-2.0 / head_size))
    positions = (first_pos + jnp.arange(row_count, dtype=jnp.int32)).astype(jnp.float32)
    angles = positions[:, None] * frequency[None, :]
    cosine_table = jnp.cos(angles)[:, None, :]
    sine_table = jnp.sin(angles)[:, None, :]
    first_half = shaped[..., :half_size]
    second_half = shaped[..., half_size:]
    turned = jnp.concatenate(
        [
            first_half * cosine_table - second_half * sine_table,
            second_half * cosine_table + first_half * sine_table,
        ],
        axis=-1,
    )
    return turned.reshape(values.shape)


def normalize(rows_in, gain):
    widened = rows_in.astype(jnp.float32)
    inverse_rms = lax.rsqrt(jnp.mean(widened * widened, axis=-1, keepdims=True) + EPSILON)
    return (widened * inverse_rms * gain.astype(jnp.float32)).astype(jnp.bfloat16)


def attend(query_block, start_row, key_rows, value_rows, length):
    row_count = query_block.shape[0]
    scores = jnp.dot(query_block, key_rows.T, preferred_element_type=jnp.float32) * key_rows.shape[
        1
    ] ** (-0.5)
    query_pos = start_row + jnp.arange(row_count, dtype=jnp.int32)[:, None]
    key_pos = jnp.arange(key_rows.shape[0], dtype=jnp.int32)[None, :]
    allowed = (key_pos <= query_pos) & (key_pos < length)
    scores = jnp.where(allowed, scores, -jnp.inf)
    row_top = jnp.max(scores, axis=-1, keepdims=True)
    powered = jnp.exp(scores - row_top)
    weights = (powered / jnp.sum(powered, axis=-1, keepdims=True)).astype(jnp.bfloat16)
    return jnp.dot(weights, value_rows, preferred_element_type=jnp.float32).astype(jnp.bfloat16)


def to_request(received, shift_by):
    rolled = jnp.roll(received, -shift_by, axis=0)
    return jnp.swapaxes(rolled, 0, 1).reshape(-1, received.shape[2])


def from_request(request_rows, shift_by, source_count):
    shaped = request_rows.reshape(-1, source_count, request_rows.shape[1])
    return jnp.roll(jnp.swapaxes(shaped, 0, 1), shift_by, axis=0)


def ring_blocks(narrow, axis_name):
    count = lax.axis_size(axis_name)
    blocks = [narrow]
    for shift in range(1, count):
        perm = [(index, (index - shift) % count) for index in range(count)]
        blocks.append(lax.ppermute(narrow, axis_name, perm))
    return blocks


def project_blocks(blocks, gain, query_weight, keyval_weight, axis_name):
    count = lax.axis_size(axis_name)
    position = lax.axis_index(axis_name)
    width = blocks[0].shape[1]
    widened = [block.astype(jnp.float32) for block in blocks]
    squares = sum(jnp.sum(block * block, axis=-1, keepdims=True) for block in widened)
    inverse_rms = lax.rsqrt(squares / (width * count) + EPSILON)
    queries = None
    keyvals = None
    for shift, block in enumerate(widened):
        first = ((position + shift) % count) * width
        block_gain = lax.dynamic_slice_in_dim(gain, first, width, 0).astype(jnp.float32)
        normed = (block * inverse_rms * block_gain).astype(jnp.bfloat16)
        query_part = jnp.dot(
            normed,
            lax.dynamic_slice_in_dim(query_weight, first, width, 0),
            preferred_element_type=jnp.float32,
        )
        keyval_part = jnp.dot(
            normed,
            lax.dynamic_slice_in_dim(keyval_weight, first, width, 0),
            preferred_element_type=jnp.float32,
        )
        queries = query_part if queries is None else queries + query_part
        keyvals = keyval_part if keyvals is None else keyvals + keyval_part
    return queries, keyvals


def ring_output(local_attention, output_weight, axis_name):
    count = lax.axis_size(axis_name)
    position = lax.axis_index(axis_name)
    width = output_weight.shape[1] // count
    total = None
    for shift in range(count):
        first = ((position + shift) % count) * width
        part = jnp.dot(
            local_attention,
            lax.dynamic_slice_in_dim(output_weight, first, width, 1),
            preferred_element_type=jnp.float32,
        ).astype(jnp.bfloat16)
        if shift == 0:
            total = part.astype(jnp.float32)
        else:
            perm = [(index, (index + shift) % count) for index in range(count)]
            total = total + lax.ppermute(part, axis_name, perm).astype(jnp.float32)
    return total.astype(jnp.bfloat16)


def body(
    hidden_in,
    norm_gain,
    query_weight,
    keyval_weight,
    output_weight,
    segment_ids,
    request_lengths,
    request_owner,
    cache_slots,
):
    source_count = lax.axis_size("seq")
    source_pos = lax.axis_index("seq")
    local_rows = hidden_in.shape[0]
    capacity = MAXLEN // source_count
    chunk_slots = capacity // CHUNKS
    chunk_rows = chunk_slots * source_count
    request_ids = jnp.arange(source_count, dtype=jnp.int32)
    starts = jnp.cumsum(request_lengths) - request_lengths
    first_row = jnp.maximum((starts - source_pos + source_count - 1) // source_count, 0)
    owner_match = request_owner[None, :] == request_ids[:, None]
    send_first = jnp.sum(jnp.where(owner_match, first_row[None, :], 0), axis=1)
    send_start = jnp.sum(jnp.where(owner_match, starts[None, :], 0), axis=1)
    send_length = jnp.sum(jnp.where(owner_match, request_lengths[None, :], 0), axis=1)
    row_index = send_first[:, None] + jnp.arange(capacity, dtype=jnp.int32)[None, :]
    stream_pos = row_index * source_count + source_pos
    live_send = (
        (row_index < local_rows)
        & (stream_pos >= send_start[:, None])
        & (stream_pos < (send_start + send_length)[:, None])
    )
    local_ids = jnp.arange(local_rows, dtype=jnp.int32)
    select = (
        (row_index.reshape(-1)[:, None] == local_ids[None, :]) & live_send.reshape(-1)[:, None]
    ).astype(jnp.bfloat16)
    send_slot = jnp.sum(jnp.where(owner_match, cache_slots[None, :], 0), axis=1)
    own_start = lax.dynamic_index_in_dim(send_start, source_pos, 0, keepdims=False)
    own_length = lax.dynamic_index_in_dim(send_length, source_pos, 0, keepdims=False)
    own_slot = lax.dynamic_index_in_dim(send_slot, source_pos, 0, keepdims=False)
    shift_by = own_start % source_count
    picked = (
        jnp.dot(select, hidden_in, preferred_element_type=jnp.float32)
        .astype(jnp.bfloat16)
        .reshape(source_count, capacity, hidden_in.shape[1])
    )
    head_count = query_weight.shape[1] // HD
    per_group = HEADS // KV_HEADS
    block_count = keyval_weight.shape[1] // HD
    key_chunks = []
    value_chunks = []
    cached_chunks = []
    returned_chunks = []
    for chunk in range(CHUNKS):
        chunk_first = chunk * chunk_rows
        arrived = lax.all_to_all(
            picked[:, chunk * chunk_slots : (chunk + 1) * chunk_slots],
            "seq",
            split_axis=0,
            concat_axis=0,
            tiled=True,
        )
        narrow_rows = to_request(arrived, shift_by)
        queries, keyvals = project_blocks(
            ring_blocks(narrow_rows, "tensor"), norm_gain, query_weight, keyval_weight, "tensor"
        )
        rotated_query = rotate_rows(queries, HD, chunk_first).astype(jnp.bfloat16)
        own_blocks = []
        for block_index in range(block_count):
            plain_block = keyvals[:, block_index * HD : (block_index + 1) * HD]
            if block_index % 2 == 0:
                own_blocks.append(rotate_rows(plain_block, HD, chunk_first).astype(jnp.bfloat16))
            else:
                own_blocks.append(plain_block.astype(jnp.bfloat16))
        own_cached = jnp.concatenate(own_blocks, axis=1)
        cached_chunks.append(own_cached)
        key_chunks.append(own_cached[:, 0:HD])
        value_chunks.append(own_cached[:, HD : 2 * HD])
        key_rows = jnp.concatenate(key_chunks, axis=0)
        value_rows = jnp.concatenate(value_chunks, axis=0)
        head_outputs = []
        for head_index in range(head_count):
            head_outputs.append(
                attend(
                    rotated_query[:, head_index * HD : (head_index + 1) * HD],
                    chunk_first,
                    key_rows,
                    value_rows,
                    own_length,
                )
            )
        attention_rows = jnp.concatenate(head_outputs, axis=1)
        outgoing = from_request(attention_rows, shift_by, source_count)
        returned_chunks.append(
            lax.all_to_all(outgoing, "seq", split_axis=0, concat_axis=0, tiled=True)
        )
    returned = jnp.concatenate(returned_chunks, axis=1)
    flattened = returned.reshape(-1, returned.shape[2])
    local_attention = lax.dot_general(
        select, flattened, (((0,), (0,)), ((), ())), preferred_element_type=jnp.float32
    ).astype(jnp.bfloat16)
    attended = ring_output(local_attention, output_weight, "tensor")
    all_cached = jnp.concatenate(cached_chunks, axis=0)
    slot_ids = jnp.arange(SLOTS_DEV, dtype=jnp.int32)
    cache_table = jnp.where(
        (slot_ids == own_slot)[:, None, None], all_cached[None], jnp.zeros((), jnp.bfloat16)
    )
    return (attended, cache_table)


def solution(mesh):
    in_specs = (
        P("seq", "tensor"),
        P(),
        P(None, "tensor"),
        P(None, "tensor"),
        P("tensor", None),
        P("seq"),
        P(),
        P(),
        P(),
    )
    out_specs = (P("seq", "tensor"), P("seq", None, "tensor"))
    return jax.shard_map(body, mesh=mesh, in_specs=in_specs, out_specs=out_specs, check_vma=False)
```

```python
import jax
import jax.numpy as jnp
from jax import lax
from jax.sharding import PartitionSpec as P

HEADS = 8
KV_HEADS = 4
HD = 256
SLOTS_DEV = 2
MAXLEN = 512
FILLED = 28672


EPSILON = 1e-06
ROPE_BASE = 1000042.0
CHUNKS = 1


def rotate_rows(values, head_size, first_pos):
    row_count = values.shape[0]
    shaped = values.reshape(row_count, -1, head_size)
    half_size = head_size // 2
    frequency = ROPE_BASE ** (jnp.arange(half_size, dtype=jnp.float32) * (-2.0 / head_size))
    positions = (first_pos + jnp.arange(row_count, dtype=jnp.int32)).astype(jnp.float32)
    angles = positions[:, None] * frequency[None, :]
    cosine_table = jnp.cos(angles)[:, None, :]
    sine_table = jnp.sin(angles)[:, None, :]
    first_half = shaped[..., :half_size]
    second_half = shaped[..., half_size:]
    turned = jnp.concatenate(
        [
            first_half * cosine_table - second_half * sine_table,
            second_half * cosine_table + first_half * sine_table,
        ],
        axis=-1,
    )
    return turned.reshape(values.shape)


def normalize(rows_in, gain):
    widened = rows_in.astype(jnp.float32)
    inverse_rms = lax.rsqrt(jnp.mean(widened * widened, axis=-1, keepdims=True) + EPSILON)
    return (widened * inverse_rms * gain.astype(jnp.float32)).astype(jnp.bfloat16)


def attend(query_block, start_row, key_rows, value_rows, length):
    row_count = query_block.shape[0]
    scores = jnp.dot(query_block, key_rows.T, preferred_element_type=jnp.float32) * key_rows.shape[
        1
    ] ** (-0.5)
    query_pos = start_row + jnp.arange(row_count, dtype=jnp.int32)[:, None]
    key_pos = jnp.arange(key_rows.shape[0], dtype=jnp.int32)[None, :]
    allowed = (key_pos <= query_pos) & (key_pos < length)
    scores = jnp.where(allowed, scores, -jnp.inf)
    row_top = jnp.max(scores, axis=-1, keepdims=True)
    powered = jnp.exp(scores - row_top)
    weights = (powered / jnp.sum(powered, axis=-1, keepdims=True)).astype(jnp.bfloat16)
    return jnp.dot(weights, value_rows, preferred_element_type=jnp.float32).astype(jnp.bfloat16)


def to_request(received, shift_by):
    rolled = jnp.roll(received, -shift_by, axis=0)
    return jnp.swapaxes(rolled, 0, 1).reshape(-1, received.shape[2])


def from_request(request_rows, shift_by, source_count):
    shaped = request_rows.reshape(-1, source_count, request_rows.shape[1])
    return jnp.roll(jnp.swapaxes(shaped, 0, 1), shift_by, axis=0)


def ring_blocks(narrow, axis_name):
    count = lax.axis_size(axis_name)
    blocks = [narrow]
    for shift in range(1, count):
        perm = [(index, (index - shift) % count) for index in range(count)]
        blocks.append(lax.ppermute(narrow, axis_name, perm))
    return blocks


def project_blocks(blocks, gain, query_weight, keyval_weight, axis_name):
    count = lax.axis_size(axis_name)
    position = lax.axis_index(axis_name)
    width = blocks[0].shape[1]
    widened = [block.astype(jnp.float32) for block in blocks]
    squares = sum(jnp.sum(block * block, axis=-1, keepdims=True) for block in widened)
    inverse_rms = lax.rsqrt(squares / (width * count) + EPSILON)
    queries = None
    keyvals = None
    for shift, block in enumerate(widened):
        first = ((position + shift) % count) * width
        block_gain = lax.dynamic_slice_in_dim(gain, first, width, 0).astype(jnp.float32)
        normed = (block * inverse_rms * block_gain).astype(jnp.bfloat16)
        query_part = jnp.dot(
            normed,
            lax.dynamic_slice_in_dim(query_weight, first, width, 0),
            preferred_element_type=jnp.float32,
        )
        keyval_part = jnp.dot(
            normed,
            lax.dynamic_slice_in_dim(keyval_weight, first, width, 0),
            preferred_element_type=jnp.float32,
        )
        queries = query_part if queries is None else queries + query_part
        keyvals = keyval_part if keyvals is None else keyvals + keyval_part
    return queries, keyvals


def ring_output(local_attention, output_weight, axis_name):
    count = lax.axis_size(axis_name)
    position = lax.axis_index(axis_name)
    width = output_weight.shape[1] // count
    total = None
    for shift in range(count):
        first = ((position + shift) % count) * width
        part = jnp.dot(
            local_attention,
            lax.dynamic_slice_in_dim(output_weight, first, width, 1),
            preferred_element_type=jnp.float32,
        ).astype(jnp.bfloat16)
        if shift == 0:
            total = part.astype(jnp.float32)
        else:
            perm = [(index, (index + shift) % count) for index in range(count)]
            total = total + lax.ppermute(part, axis_name, perm).astype(jnp.float32)
    return total.astype(jnp.bfloat16)


def body(
    hidden_in,
    norm_gain,
    query_weight,
    keyval_weight,
    output_weight,
    segment_ids,
    request_lengths,
    request_owner,
    cache_slots,
):
    source_count = lax.axis_size("seq")
    source_pos = lax.axis_index("seq")
    local_rows = hidden_in.shape[0]
    capacity = MAXLEN // source_count
    chunk_slots = capacity // CHUNKS
    chunk_rows = chunk_slots * source_count
    request_ids = jnp.arange(source_count, dtype=jnp.int32)
    starts = jnp.cumsum(request_lengths) - request_lengths
    first_row = jnp.maximum((starts - source_pos + source_count - 1) // source_count, 0)
    owner_match = request_owner[None, :] == request_ids[:, None]
    send_first = jnp.sum(jnp.where(owner_match, first_row[None, :], 0), axis=1)
    send_start = jnp.sum(jnp.where(owner_match, starts[None, :], 0), axis=1)
    send_length = jnp.sum(jnp.where(owner_match, request_lengths[None, :], 0), axis=1)
    row_index = send_first[:, None] + jnp.arange(capacity, dtype=jnp.int32)[None, :]
    stream_pos = row_index * source_count + source_pos
    live_send = (
        (row_index < local_rows)
        & (stream_pos >= send_start[:, None])
        & (stream_pos < (send_start + send_length)[:, None])
    )
    local_ids = jnp.arange(local_rows, dtype=jnp.int32)
    select = (
        (row_index.reshape(-1)[:, None] == local_ids[None, :]) & live_send.reshape(-1)[:, None]
    ).astype(jnp.bfloat16)
    send_slot = jnp.sum(jnp.where(owner_match, cache_slots[None, :], 0), axis=1)
    own_start = lax.dynamic_index_in_dim(send_start, source_pos, 0, keepdims=False)
    own_length = lax.dynamic_index_in_dim(send_length, source_pos, 0, keepdims=False)
    own_slot = lax.dynamic_index_in_dim(send_slot, source_pos, 0, keepdims=False)
    shift_by = own_start % source_count
    picked = (
        jnp.dot(select, hidden_in, preferred_element_type=jnp.float32)
        .astype(jnp.bfloat16)
        .reshape(source_count, capacity, hidden_in.shape[1])
    )
    head_count = query_weight.shape[1] // HD
    per_group = HEADS // KV_HEADS
    block_count = keyval_weight.shape[1] // HD
    key_chunks = []
    value_chunks = []
    cached_chunks = []
    returned_chunks = []
    for chunk in range(CHUNKS):
        chunk_first = chunk * chunk_rows
        arrived = lax.all_to_all(
            picked[:, chunk * chunk_slots : (chunk + 1) * chunk_slots],
            "seq",
            split_axis=0,
            concat_axis=0,
            tiled=True,
        )
        narrow_rows = to_request(arrived, shift_by)
        queries, keyvals = project_blocks(
            ring_blocks(narrow_rows, "tensor"), norm_gain, query_weight, keyval_weight, "tensor"
        )
        rotated_query = rotate_rows(queries, HD, chunk_first).astype(jnp.bfloat16)
        own_blocks = []
        for block_index in range(block_count):
            plain_block = keyvals[:, block_index * HD : (block_index + 1) * HD]
            if block_index % 2 == 0:
                own_blocks.append(rotate_rows(plain_block, HD, chunk_first).astype(jnp.bfloat16))
            else:
                own_blocks.append(plain_block.astype(jnp.bfloat16))
        own_cached = jnp.concatenate(own_blocks, axis=1)
        cached_chunks.append(own_cached)
        key_chunks.append(own_cached[:, 0:HD])
        value_chunks.append(own_cached[:, HD : 2 * HD])
        key_rows = jnp.concatenate(key_chunks, axis=0)
        value_rows = jnp.concatenate(value_chunks, axis=0)
        head_outputs = []
        for head_index in range(head_count):
            head_outputs.append(
                attend(
                    rotated_query[:, head_index * HD : (head_index + 1) * HD],
                    chunk_first,
                    key_rows,
                    value_rows,
                    own_length,
                )
            )
        attention_rows = jnp.concatenate(head_outputs, axis=1)
        outgoing = from_request(attention_rows, shift_by, source_count)
        returned_chunks.append(
            lax.all_to_all(outgoing, "seq", split_axis=0, concat_axis=0, tiled=True)
        )
    returned = jnp.concatenate(returned_chunks, axis=1)
    flattened = returned.reshape(-1, returned.shape[2])
    local_attention = lax.dot_general(
        select, flattened, (((0,), (0,)), ((), ())), preferred_element_type=jnp.float32
    ).astype(jnp.bfloat16)
    filled_rows = min(-(-FILLED // source_count), local_rows)
    attended = ring_output(local_attention[:filled_rows], output_weight, "tensor")
    if filled_rows < local_rows:
        attended = jnp.concatenate(
            [attended, jnp.zeros((local_rows - filled_rows, attended.shape[1]), attended.dtype)],
            axis=0,
        )
    all_cached = jnp.concatenate(cached_chunks, axis=0)
    slot_ids = jnp.arange(SLOTS_DEV, dtype=jnp.int32)
    cache_table = jnp.where(
        (slot_ids == own_slot)[:, None, None], all_cached[None], jnp.zeros((), jnp.bfloat16)
    )
    return (attended, cache_table)


def solution(mesh):
    in_specs = (
        P("seq", "tensor"),
        P(),
        P(None, "tensor"),
        P(None, "tensor"),
        P("tensor", None),
        P("seq"),
        P(),
        P(),
        P(),
    )
    out_specs = (P("seq", "tensor"), P("seq", None, "tensor"))
    return jax.shard_map(body, mesh=mesh, in_specs=in_specs, out_specs=out_specs, check_vma=False)
```

```python
import jax
import jax.numpy as jnp
from jax import lax
from jax.sharding import PartitionSpec as P

HEADS = 8
KV_HEADS = 4
HD = 256
SLOTS_DEV = 2
MAXLEN = 512
FILLED = 28672


EPSILON = 1e-06
ROPE_BASE = 1000042.0
CHUNKS = 1


def rotate_rows(values, head_size, row_pos):
    row_count = values.shape[0]
    shaped = values.reshape(row_count, -1, head_size)
    half_size = head_size // 2
    frequency = ROPE_BASE ** (jnp.arange(half_size, dtype=jnp.float32) * (-2.0 / head_size))
    positions = row_pos.astype(jnp.float32)
    angles = positions[:, None] * frequency[None, :]
    cosine_table = jnp.cos(angles)[:, None, :]
    sine_table = jnp.sin(angles)[:, None, :]
    first_half = shaped[..., :half_size]
    second_half = shaped[..., half_size:]
    turned = jnp.concatenate(
        [
            first_half * cosine_table - second_half * sine_table,
            second_half * cosine_table + first_half * sine_table,
        ],
        axis=-1,
    )
    return turned.reshape(values.shape)


def normalize(rows_in, gain):
    widened = rows_in.astype(jnp.float32)
    inverse_rms = lax.rsqrt(jnp.mean(widened * widened, axis=-1, keepdims=True) + EPSILON)
    return (widened * inverse_rms * gain.astype(jnp.float32)).astype(jnp.bfloat16)


def attend(query_block, query_pos, key_rows, key_pos, value_rows, length):
    scores = jnp.dot(query_block, key_rows.T, preferred_element_type=jnp.float32) * key_rows.shape[
        1
    ] ** (-0.5)
    allowed = (key_pos[None, :] <= query_pos[:, None]) & (key_pos[None, :] < length)
    scores = jnp.where(allowed, scores, -jnp.inf)
    row_top = jnp.max(scores, axis=-1, keepdims=True)
    powered = jnp.exp(scores - row_top)
    weights = (powered / jnp.sum(powered, axis=-1, keepdims=True)).astype(jnp.bfloat16)
    return jnp.dot(weights, value_rows, preferred_element_type=jnp.float32).astype(jnp.bfloat16)


def to_request(received, shift_by):
    rolled = jnp.roll(received, -shift_by, axis=0)
    return jnp.swapaxes(rolled, 0, 1).reshape(-1, received.shape[2])


def from_request(request_rows, shift_by, source_count):
    shaped = request_rows.reshape(-1, source_count, request_rows.shape[1])
    return jnp.roll(jnp.swapaxes(shaped, 0, 1), shift_by, axis=0)


def ring_blocks(narrow, axis_name):
    count = lax.axis_size(axis_name)
    blocks = [narrow]
    for shift in range(1, count):
        perm = [(index, (index - shift) % count) for index in range(count)]
        blocks.append(lax.ppermute(narrow, axis_name, perm))
    return blocks


def project_blocks(blocks, gain, query_weight, keyval_weight, axis_name):
    count = lax.axis_size(axis_name)
    position = lax.axis_index(axis_name)
    width = blocks[0].shape[1]
    widened = [block.astype(jnp.float32) for block in blocks]
    squares = sum(jnp.sum(block * block, axis=-1, keepdims=True) for block in widened)
    inverse_rms = lax.rsqrt(squares / (width * count) + EPSILON)
    queries = None
    keyvals = None
    for shift, block in enumerate(widened):
        first = ((position + shift) % count) * width
        block_gain = lax.dynamic_slice_in_dim(gain, first, width, 0).astype(jnp.float32)
        normed = (block * inverse_rms * block_gain).astype(jnp.bfloat16)
        query_part = jnp.dot(
            normed,
            lax.dynamic_slice_in_dim(query_weight, first, width, 0),
            preferred_element_type=jnp.float32,
        )
        keyval_part = jnp.dot(
            normed,
            lax.dynamic_slice_in_dim(keyval_weight, first, width, 0),
            preferred_element_type=jnp.float32,
        )
        queries = query_part if queries is None else queries + query_part
        keyvals = keyval_part if keyvals is None else keyvals + keyval_part
    return queries, keyvals


def ring_output(local_attention, output_weight, axis_name):
    count = lax.axis_size(axis_name)
    position = lax.axis_index(axis_name)
    width = output_weight.shape[1] // count
    total = None
    for shift in range(count):
        first = ((position + shift) % count) * width
        part = jnp.dot(
            local_attention,
            lax.dynamic_slice_in_dim(output_weight, first, width, 1),
            preferred_element_type=jnp.float32,
        ).astype(jnp.bfloat16)
        if shift == 0:
            total = part.astype(jnp.float32)
        else:
            perm = [(index, (index + shift) % count) for index in range(count)]
            total = total + lax.ppermute(part, axis_name, perm).astype(jnp.float32)
    return total.astype(jnp.bfloat16)


def body(
    hidden_in,
    norm_gain,
    query_weight,
    keyval_weight,
    output_weight,
    segment_ids,
    request_lengths,
    request_owner,
    cache_slots,
):
    source_count = lax.axis_size("seq")
    source_pos = lax.axis_index("seq")
    local_rows = hidden_in.shape[0]
    capacity = MAXLEN // source_count
    chunk_slots = capacity // CHUNKS
    chunk_rows = chunk_slots * source_count
    request_ids = jnp.arange(source_count, dtype=jnp.int32)
    starts = jnp.cumsum(request_lengths) - request_lengths
    first_row = jnp.maximum((starts - source_pos + source_count - 1) // source_count, 0)
    owner_match = request_owner[None, :] == request_ids[:, None]
    send_first = jnp.sum(jnp.where(owner_match, first_row[None, :], 0), axis=1)
    send_start = jnp.sum(jnp.where(owner_match, starts[None, :], 0), axis=1)
    send_length = jnp.sum(jnp.where(owner_match, request_lengths[None, :], 0), axis=1)
    row_index = send_first[:, None] + jnp.arange(capacity, dtype=jnp.int32)[None, :]
    stream_pos = row_index * source_count + source_pos
    live_send = (
        (row_index < local_rows)
        & (stream_pos >= send_start[:, None])
        & (stream_pos < (send_start + send_length)[:, None])
    )
    local_ids = jnp.arange(local_rows, dtype=jnp.int32)
    select = (
        (row_index.reshape(-1)[:, None] == local_ids[None, :]) & live_send.reshape(-1)[:, None]
    ).astype(jnp.bfloat16)
    send_slot = jnp.sum(jnp.where(owner_match, cache_slots[None, :], 0), axis=1)
    own_start = lax.dynamic_index_in_dim(send_start, source_pos, 0, keepdims=False)
    own_length = lax.dynamic_index_in_dim(send_length, source_pos, 0, keepdims=False)
    own_slot = lax.dynamic_index_in_dim(send_slot, source_pos, 0, keepdims=False)
    shift_by = own_start % source_count
    picked = (
        jnp.dot(select, hidden_in, preferred_element_type=jnp.float32)
        .astype(jnp.bfloat16)
        .reshape(source_count, capacity, hidden_in.shape[1])
    )
    head_count = query_weight.shape[1] // HD
    per_group = HEADS // KV_HEADS
    block_count = keyval_weight.shape[1] // HD
    key_chunks = []
    value_chunks = []
    cached_chunks = []
    returned_chunks = []
    pos_chunks = []
    for chunk in range(CHUNKS):
        chunk_first = chunk * chunk_rows
        arrived = lax.all_to_all(
            picked[:, chunk * chunk_slots : (chunk + 1) * chunk_slots],
            "seq",
            split_axis=0,
            concat_axis=0,
            tiled=True,
        )
        narrow_rows = arrived.reshape(-1, arrived.shape[2])
        source_ids = jnp.arange(source_count, dtype=jnp.int32)
        chunk_pos = (
            (source_ids[:, None] - shift_by) % source_count
            + (chunk * chunk_slots + jnp.arange(chunk_slots, dtype=jnp.int32))[None, :] * source_count
        ).reshape(-1)
        pos_chunks.append(chunk_pos)
        queries, keyvals = project_blocks(
            ring_blocks(narrow_rows, "tensor"), norm_gain, query_weight, keyval_weight, "tensor"
        )
        rotated_query = rotate_rows(queries, HD, chunk_pos).astype(jnp.bfloat16)
        own_blocks = []
        for block_index in range(block_count):
            plain_block = keyvals[:, block_index * HD : (block_index + 1) * HD]
            if block_index % 2 == 0:
                own_blocks.append(rotate_rows(plain_block, HD, chunk_pos).astype(jnp.bfloat16))
            else:
                own_blocks.append(plain_block.astype(jnp.bfloat16))
        own_cached = jnp.concatenate(own_blocks, axis=1)
        cached_chunks.append(own_cached)
        key_chunks.append(own_cached[:, 0:HD])
        value_chunks.append(own_cached[:, HD : 2 * HD])
        key_rows = jnp.concatenate(key_chunks, axis=0)
        value_rows = jnp.concatenate(value_chunks, axis=0)
        head_outputs = []
        for head_index in range(head_count):
            head_outputs.append(
                attend(
                    rotated_query[:, head_index * HD : (head_index + 1) * HD],
                    chunk_pos,
                    key_rows,
                    jnp.concatenate(pos_chunks, axis=0),
                    value_rows,
                    own_length,
                )
            )
        attention_rows = jnp.concatenate(head_outputs, axis=1)
        outgoing = attention_rows.reshape(source_count, chunk_slots, attention_rows.shape[1])
        returned_chunks.append(
            lax.all_to_all(outgoing, "seq", split_axis=0, concat_axis=0, tiled=True)
        )
    returned = jnp.concatenate(returned_chunks, axis=1)
    flattened = returned.reshape(-1, returned.shape[2])
    local_attention = lax.dot_general(
        select, flattened, (((0,), (0,)), ((), ())), preferred_element_type=jnp.float32
    ).astype(jnp.bfloat16)
    filled_rows = min(-(-FILLED // source_count), local_rows)
    attended = ring_output(local_attention[:filled_rows], output_weight, "tensor")
    if filled_rows < local_rows:
        attended = jnp.concatenate(
            [attended, jnp.zeros((local_rows - filled_rows, attended.shape[1]), attended.dtype)],
            axis=0,
        )
    all_cached = to_request(
        jnp.concatenate(
            [block.reshape(source_count, chunk_slots, -1) for block in cached_chunks], axis=1
        ),
        shift_by,
    )
    slot_ids = jnp.arange(SLOTS_DEV, dtype=jnp.int32)
    cache_table = jnp.where(
        (slot_ids == own_slot)[:, None, None], all_cached[None], jnp.zeros((), jnp.bfloat16)
    )
    return (attended, cache_table)


def solution(mesh):
    in_specs = (
        P("seq", "tensor"),
        P(),
        P(None, "tensor"),
        P(None, "tensor"),
        P("tensor", None),
        P("seq"),
        P(),
        P(),
        P(),
    )
    out_specs = (P("seq", "tensor"), P("seq", None, "tensor"))
    return jax.shard_map(body, mesh=mesh, in_specs=in_specs, out_specs=out_specs, check_vma=False)
```

```python
import jax
import jax.numpy as jnp
from jax import lax
from jax.sharding import PartitionSpec as P

HEADS = 8
KV_HEADS = 4
HD = 256
SLOTS_DEV = 2
MAXLEN = 512
FILLED = 28672


EPSILON = 1e-06
ROPE_BASE = 1000042.0
CHUNKS = 1


def rotate_rows(values, head_size, first_pos):
    row_count = values.shape[0]
    shaped = values.reshape(row_count, -1, head_size)
    half_size = head_size // 2
    frequency = ROPE_BASE ** (jnp.arange(half_size, dtype=jnp.float32) * (-2.0 / head_size))
    positions = (first_pos + jnp.arange(row_count, dtype=jnp.int32)).astype(jnp.float32)
    angles = positions[:, None] * frequency[None, :]
    cosine_table = jnp.cos(angles)[:, None, :]
    sine_table = jnp.sin(angles)[:, None, :]
    first_half = shaped[..., :half_size]
    second_half = shaped[..., half_size:]
    turned = jnp.concatenate(
        [
            first_half * cosine_table - second_half * sine_table,
            second_half * cosine_table + first_half * sine_table,
        ],
        axis=-1,
    )
    return turned.reshape(values.shape)


def normalize(rows_in, gain):
    widened = rows_in.astype(jnp.float32)
    inverse_rms = lax.rsqrt(jnp.mean(widened * widened, axis=-1, keepdims=True) + EPSILON)
    return (widened * inverse_rms * gain.astype(jnp.float32)).astype(jnp.bfloat16)


def attend(query_block, start_row, key_rows, value_rows, length):
    row_count = query_block.shape[0]
    scores = jnp.dot(query_block, key_rows.T, preferred_element_type=jnp.float32) * key_rows.shape[
        1
    ] ** (-0.5)
    query_pos = start_row + jnp.arange(row_count, dtype=jnp.int32)[:, None]
    key_pos = jnp.arange(key_rows.shape[0], dtype=jnp.int32)[None, :]
    allowed = (key_pos <= query_pos) & (key_pos < length)
    scores = jnp.where(allowed, scores, -jnp.inf)
    row_top = jnp.max(scores, axis=-1, keepdims=True)
    powered = jnp.exp(scores - row_top)
    weights = (powered / jnp.sum(powered, axis=-1, keepdims=True)).astype(jnp.bfloat16)
    return jnp.dot(weights, value_rows, preferred_element_type=jnp.float32).astype(jnp.bfloat16)


def to_request(received, shift_by):
    rolled = jnp.roll(received, -shift_by, axis=0)
    return jnp.swapaxes(rolled, 0, 1).reshape(-1, received.shape[2])


def from_request(request_rows, shift_by, source_count):
    shaped = request_rows.reshape(-1, source_count, request_rows.shape[1])
    return jnp.roll(jnp.swapaxes(shaped, 0, 1), shift_by, axis=0)


def ring_blocks(narrow, axis_name):
    count = lax.axis_size(axis_name)
    blocks = [narrow]
    for shift in range(1, count):
        perm = [(index, (index - shift) % count) for index in range(count)]
        blocks.append(lax.ppermute(narrow, axis_name, perm))
    return blocks


def project_blocks(blocks, gain, query_weight, keyval_weight, axis_name):
    count = lax.axis_size(axis_name)
    position = lax.axis_index(axis_name)
    width = blocks[0].shape[1]
    widened = [block.astype(jnp.float32) for block in blocks]
    squares = sum(jnp.sum(block * block, axis=-1, keepdims=True) for block in widened)
    inverse_rms = lax.rsqrt(squares / (width * count) + EPSILON)
    queries = None
    keyvals = None
    for shift, block in enumerate(widened):
        first = ((position + shift) % count) * width
        block_gain = lax.dynamic_slice_in_dim(gain, first, width, 0).astype(jnp.float32)
        normed = (block * inverse_rms * block_gain).astype(jnp.bfloat16)
        query_part = jnp.dot(
            normed,
            lax.dynamic_slice_in_dim(query_weight, first, width, 0),
            preferred_element_type=jnp.float32,
        )
        keyval_part = jnp.dot(
            normed,
            lax.dynamic_slice_in_dim(keyval_weight, first, width, 0),
            preferred_element_type=jnp.float32,
        )
        queries = query_part if queries is None else queries + query_part
        keyvals = keyval_part if keyvals is None else keyvals + keyval_part
    return queries, keyvals


def ring_output(local_attention, output_weight, axis_name):
    count = lax.axis_size(axis_name)
    position = lax.axis_index(axis_name)
    width = output_weight.shape[1] // count
    total = None
    for shift in range(count):
        first = ((position + shift) % count) * width
        part = jnp.dot(
            local_attention,
            lax.dynamic_slice_in_dim(output_weight, first, width, 1),
            preferred_element_type=jnp.float32,
        ).astype(jnp.bfloat16)
        if shift == 0:
            total = part.astype(jnp.float32)
        else:
            perm = [(index, (index + shift) % count) for index in range(count)]
            total = total + lax.ppermute(part, axis_name, perm).astype(jnp.float32)
    return total.astype(jnp.bfloat16)


def body(
    hidden_in,
    norm_gain,
    query_weight,
    keyval_weight,
    output_weight,
    segment_ids,
    request_lengths,
    request_owner,
    cache_slots,
):
    source_count = lax.axis_size("seq")
    source_pos = lax.axis_index("seq")
    local_rows = hidden_in.shape[0]
    capacity = MAXLEN // source_count
    chunk_slots = capacity // CHUNKS
    chunk_rows = chunk_slots * source_count
    request_ids = jnp.arange(source_count, dtype=jnp.int32)
    starts = jnp.sum(
        jnp.where(request_ids[None, :] < request_ids[:, None], request_lengths[None, :], 0), axis=1
    )
    first_row = jnp.maximum((starts - source_pos + source_count - 1) // source_count, 0)
    owner_match = request_owner[None, :] == request_ids[:, None]
    send_first = jnp.sum(jnp.where(owner_match, first_row[None, :], 0), axis=1)
    send_start = jnp.sum(jnp.where(owner_match, starts[None, :], 0), axis=1)
    send_length = jnp.sum(jnp.where(owner_match, request_lengths[None, :], 0), axis=1)
    row_index = send_first[:, None] + jnp.arange(capacity, dtype=jnp.int32)[None, :]
    stream_pos = row_index * source_count + source_pos
    live_send = (
        (row_index < local_rows)
        & (stream_pos >= send_start[:, None])
        & (stream_pos < (send_start + send_length)[:, None])
    )
    local_ids = jnp.arange(local_rows, dtype=jnp.int32)
    select = (
        (row_index.reshape(-1)[:, None] == local_ids[None, :]) & live_send.reshape(-1)[:, None]
    ).astype(jnp.bfloat16)
    send_slot = jnp.sum(jnp.where(owner_match, cache_slots[None, :], 0), axis=1)
    own_start = lax.dynamic_index_in_dim(send_start, source_pos, 0, keepdims=False)
    own_length = lax.dynamic_index_in_dim(send_length, source_pos, 0, keepdims=False)
    own_slot = lax.dynamic_index_in_dim(send_slot, source_pos, 0, keepdims=False)
    shift_by = own_start % source_count
    picked = (
        jnp.dot(select, hidden_in, preferred_element_type=jnp.float32)
        .astype(jnp.bfloat16)
        .reshape(source_count, capacity, hidden_in.shape[1])
    )
    head_count = query_weight.shape[1] // HD
    per_group = HEADS // KV_HEADS
    block_count = keyval_weight.shape[1] // HD
    key_chunks = []
    value_chunks = []
    cached_chunks = []
    returned_chunks = []
    for chunk in range(CHUNKS):
        chunk_first = chunk * chunk_rows
        arrived = lax.all_to_all(
            picked[:, chunk * chunk_slots : (chunk + 1) * chunk_slots],
            "seq",
            split_axis=0,
            concat_axis=0,
            tiled=True,
        )
        narrow_rows = to_request(arrived, shift_by)
        queries, keyvals = project_blocks(
            ring_blocks(narrow_rows, "tensor"), norm_gain, query_weight, keyval_weight, "tensor"
        )
        rotated_query = rotate_rows(queries, HD, chunk_first).astype(jnp.bfloat16)
        own_blocks = []
        for block_index in range(block_count):
            plain_block = keyvals[:, block_index * HD : (block_index + 1) * HD]
            if block_index % 2 == 0:
                own_blocks.append(rotate_rows(plain_block, HD, chunk_first).astype(jnp.bfloat16))
            else:
                own_blocks.append(plain_block.astype(jnp.bfloat16))
        own_cached = jnp.concatenate(own_blocks, axis=1)
        cached_chunks.append(own_cached)
        key_chunks.append(own_cached[:, 0:HD])
        value_chunks.append(own_cached[:, HD : 2 * HD])
        key_rows = jnp.concatenate(key_chunks, axis=0)
        value_rows = jnp.concatenate(value_chunks, axis=0)
        head_outputs = []
        for head_index in range(head_count):
            head_outputs.append(
                attend(
                    rotated_query[:, head_index * HD : (head_index + 1) * HD],
                    chunk_first,
                    key_rows,
                    value_rows,
                    own_length,
                )
            )
        attention_rows = jnp.concatenate(head_outputs, axis=1)
        outgoing = from_request(attention_rows, shift_by, source_count)
        returned_chunks.append(
            lax.all_to_all(outgoing, "seq", split_axis=0, concat_axis=0, tiled=True)
        )
    returned = jnp.concatenate(returned_chunks, axis=1)
    flattened = returned.reshape(-1, returned.shape[2])
    local_attention = lax.dot_general(
        select, flattened, (((0,), (0,)), ((), ())), preferred_element_type=jnp.float32
    ).astype(jnp.bfloat16)
    filled_rows = min(-(-FILLED // source_count), local_rows)
    attended = ring_output(local_attention[:filled_rows], output_weight, "tensor")
    if filled_rows < local_rows:
        attended = jnp.concatenate(
            [attended, jnp.zeros((local_rows - filled_rows, attended.shape[1]), attended.dtype)],
            axis=0,
        )
    all_cached = jnp.concatenate(cached_chunks, axis=0)
    slot_ids = jnp.arange(SLOTS_DEV, dtype=jnp.int32)
    cache_table = jnp.where(
        (slot_ids == own_slot)[:, None, None], all_cached[None], jnp.zeros((), jnp.bfloat16)
    )
    return (attended, cache_table)


def solution(mesh):
    in_specs = (
        P("seq", "tensor"),
        P(),
        P(None, "tensor"),
        P(None, "tensor"),
        P("tensor", None),
        P("seq"),
        P(),
        P(),
        P(),
    )
    out_specs = (P("seq", "tensor"), P("seq", None, "tensor"))
    return jax.shard_map(body, mesh=mesh, in_specs=in_specs, out_specs=out_specs, check_vma=False)
```

```python
import jax
import jax.numpy as jnp
from jax import lax
from jax.sharding import PartitionSpec as P

HEADS = 8
KV_HEADS = 4
HD = 256
SLOTS_DEV = 2
MAXLEN = 512
FILLED = 28672


EPSILON = 1e-06
ROPE_BASE = 1000042.0
CHUNKS = 1


def rotate_rows(values, head_size, first_pos):
    row_count = values.shape[0]
    shaped = values.reshape(row_count, -1, head_size)
    half_size = head_size // 2
    frequency = ROPE_BASE ** (jnp.arange(half_size, dtype=jnp.float32) * (-2.0 / head_size))
    positions = (first_pos + jnp.arange(row_count, dtype=jnp.int32)).astype(jnp.float32)
    angles = positions[:, None] * frequency[None, :]
    cosine_table = jnp.cos(angles)[:, None, :]
    sine_table = jnp.sin(angles)[:, None, :]
    first_half = shaped[..., :half_size]
    second_half = shaped[..., half_size:]
    turned = jnp.concatenate(
        [
            first_half * cosine_table - second_half * sine_table,
            second_half * cosine_table + first_half * sine_table,
        ],
        axis=-1,
    )
    return turned.reshape(values.shape)


def normalize(rows_in, gain):
    widened = rows_in.astype(jnp.float32)
    inverse_rms = lax.rsqrt(jnp.mean(widened * widened, axis=-1, keepdims=True) + EPSILON)
    return (widened * inverse_rms * gain.astype(jnp.float32)).astype(jnp.bfloat16)


def attend(query_block, start_row, key_rows, value_rows, length):
    row_count = query_block.shape[0]
    scores = jnp.dot(query_block, key_rows.T, preferred_element_type=jnp.float32) * key_rows.shape[
        1
    ] ** (-0.5)
    query_pos = start_row + jnp.arange(row_count, dtype=jnp.int32)[:, None]
    key_pos = jnp.arange(key_rows.shape[0], dtype=jnp.int32)[None, :]
    allowed = (key_pos <= query_pos) & (key_pos < length)
    scores = jnp.where(allowed, scores, -jnp.inf)
    row_top = jnp.max(scores, axis=-1, keepdims=True)
    powered = jnp.exp(scores - row_top)
    weights = (powered / jnp.sum(powered, axis=-1, keepdims=True)).astype(jnp.bfloat16)
    return jnp.dot(weights, value_rows, preferred_element_type=jnp.float32).astype(jnp.bfloat16)


def to_request(received, shift_by):
    rolled = jnp.roll(received, -shift_by, axis=0)
    return jnp.swapaxes(rolled, 0, 1).reshape(-1, received.shape[2])


def from_request(request_rows, shift_by, source_count):
    shaped = request_rows.reshape(-1, source_count, request_rows.shape[1])
    return jnp.roll(jnp.swapaxes(shaped, 0, 1), shift_by, axis=0)


def ring_blocks(narrow, axis_name):
    count = lax.axis_size(axis_name)
    blocks = [narrow]
    for shift in range(1, count):
        perm = [(index, (index - shift) % count) for index in range(count)]
        blocks.append(lax.ppermute(narrow, axis_name, perm))
    return blocks


def project_blocks(blocks, gain, query_weight, keyval_weight, axis_name):
    position = lax.axis_index(axis_name)
    offset = position * blocks[0].shape[1]
    rows = jnp.concatenate(blocks, axis=1)
    normed = normalize(rows, jnp.roll(gain, -offset))
    queries = jnp.dot(
        normed, jnp.roll(query_weight, -offset, axis=0), preferred_element_type=jnp.float32
    )
    keyvals = jnp.dot(
        normed, jnp.roll(keyval_weight, -offset, axis=0), preferred_element_type=jnp.float32
    )
    return queries, keyvals


def ring_output(local_attention, output_weight, axis_name):
    count = lax.axis_size(axis_name)
    position = lax.axis_index(axis_name)
    width = output_weight.shape[1] // count
    total = None
    for shift in range(count):
        first = ((position + shift) % count) * width
        part = jnp.dot(
            local_attention,
            lax.dynamic_slice_in_dim(output_weight, first, width, 1),
            preferred_element_type=jnp.float32,
        ).astype(jnp.bfloat16)
        if shift == 0:
            total = part.astype(jnp.float32)
        else:
            perm = [(index, (index + shift) % count) for index in range(count)]
            total = total + lax.ppermute(part, axis_name, perm).astype(jnp.float32)
    return total.astype(jnp.bfloat16)


def body(
    hidden_in,
    norm_gain,
    query_weight,
    keyval_weight,
    output_weight,
    segment_ids,
    request_lengths,
    request_owner,
    cache_slots,
):
    source_count = lax.axis_size("seq")
    source_pos = lax.axis_index("seq")
    local_rows = hidden_in.shape[0]
    capacity = MAXLEN // source_count
    chunk_slots = capacity // CHUNKS
    chunk_rows = chunk_slots * source_count
    request_ids = jnp.arange(source_count, dtype=jnp.int32)
    starts = jnp.sum(
        jnp.where(request_ids[None, :] < request_ids[:, None], request_lengths[None, :], 0), axis=1
    )
    first_row = jnp.maximum((starts - source_pos + source_count - 1) // source_count, 0)
    owner_match = request_owner[None, :] == request_ids[:, None]
    send_first = jnp.sum(jnp.where(owner_match, first_row[None, :], 0), axis=1)
    send_start = jnp.sum(jnp.where(owner_match, starts[None, :], 0), axis=1)
    send_length = jnp.sum(jnp.where(owner_match, request_lengths[None, :], 0), axis=1)
    row_index = send_first[:, None] + jnp.arange(capacity, dtype=jnp.int32)[None, :]
    stream_pos = row_index * source_count + source_pos
    live_send = (
        (row_index < local_rows)
        & (stream_pos >= send_start[:, None])
        & (stream_pos < (send_start + send_length)[:, None])
    )
    local_ids = jnp.arange(local_rows, dtype=jnp.int32)
    select = (
        (row_index.reshape(-1)[:, None] == local_ids[None, :]) & live_send.reshape(-1)[:, None]
    ).astype(jnp.bfloat16)
    send_slot = jnp.sum(jnp.where(owner_match, cache_slots[None, :], 0), axis=1)
    own_start = lax.dynamic_index_in_dim(send_start, source_pos, 0, keepdims=False)
    own_length = lax.dynamic_index_in_dim(send_length, source_pos, 0, keepdims=False)
    own_slot = lax.dynamic_index_in_dim(send_slot, source_pos, 0, keepdims=False)
    shift_by = own_start % source_count
    picked = (
        jnp.dot(select, hidden_in, preferred_element_type=jnp.float32)
        .astype(jnp.bfloat16)
        .reshape(source_count, capacity, hidden_in.shape[1])
    )
    head_count = query_weight.shape[1] // HD
    per_group = HEADS // KV_HEADS
    block_count = keyval_weight.shape[1] // HD
    key_chunks = []
    value_chunks = []
    cached_chunks = []
    returned_chunks = []
    for chunk in range(CHUNKS):
        chunk_first = chunk * chunk_rows
        arrived = lax.all_to_all(
            picked[:, chunk * chunk_slots : (chunk + 1) * chunk_slots],
            "seq",
            split_axis=0,
            concat_axis=0,
            tiled=True,
        )
        narrow_rows = to_request(arrived, shift_by)
        queries, keyvals = project_blocks(
            ring_blocks(narrow_rows, "tensor"), norm_gain, query_weight, keyval_weight, "tensor"
        )
        rotated_query = rotate_rows(queries, HD, chunk_first).astype(jnp.bfloat16)
        own_blocks = []
        for block_index in range(block_count):
            plain_block = keyvals[:, block_index * HD : (block_index + 1) * HD]
            if block_index % 2 == 0:
                own_blocks.append(rotate_rows(plain_block, HD, chunk_first).astype(jnp.bfloat16))
            else:
                own_blocks.append(plain_block.astype(jnp.bfloat16))
        own_cached = jnp.concatenate(own_blocks, axis=1)
        cached_chunks.append(own_cached)
        key_chunks.append(own_cached[:, 0:HD])
        value_chunks.append(own_cached[:, HD : 2 * HD])
        key_rows = jnp.concatenate(key_chunks, axis=0)
        value_rows = jnp.concatenate(value_chunks, axis=0)
        head_outputs = []
        for head_index in range(head_count):
            head_outputs.append(
                attend(
                    rotated_query[:, head_index * HD : (head_index + 1) * HD],
                    chunk_first,
                    key_rows,
                    value_rows,
                    own_length,
                )
            )
        attention_rows = jnp.concatenate(head_outputs, axis=1)
        outgoing = from_request(attention_rows, shift_by, source_count)
        returned_chunks.append(
            lax.all_to_all(outgoing, "seq", split_axis=0, concat_axis=0, tiled=True)
        )
    returned = jnp.concatenate(returned_chunks, axis=1)
    flattened = returned.reshape(-1, returned.shape[2])
    local_attention = lax.dot_general(
        select, flattened, (((0,), (0,)), ((), ())), preferred_element_type=jnp.float32
    ).astype(jnp.bfloat16)
    filled_rows = min(-(-FILLED // source_count), local_rows)
    attended = ring_output(local_attention[:filled_rows], output_weight, "tensor")
    if filled_rows < local_rows:
        attended = jnp.concatenate(
            [attended, jnp.zeros((local_rows - filled_rows, attended.shape[1]), attended.dtype)],
            axis=0,
        )
    all_cached = jnp.concatenate(cached_chunks, axis=0)
    slot_ids = jnp.arange(SLOTS_DEV, dtype=jnp.int32)
    cache_table = jnp.where(
        (slot_ids == own_slot)[:, None, None], all_cached[None], jnp.zeros((), jnp.bfloat16)
    )
    return (attended, cache_table)


def solution(mesh):
    in_specs = (
        P("seq", "tensor"),
        P(),
        P(None, "tensor"),
        P(None, "tensor"),
        P("tensor", None),
        P("seq"),
        P(),
        P(),
        P(),
    )
    out_specs = (P("seq", "tensor"), P("seq", None, "tensor"))
    return jax.shard_map(body, mesh=mesh, in_specs=in_specs, out_specs=out_specs, check_vma=False)
```

```python
import jax
import jax.numpy as jnp
from jax import lax
from jax.sharding import PartitionSpec as P

HEADS = 8
KV_HEADS = 4
HD = 256
SLOTS_DEV = 2
MAXLEN = 512
FILLED = 28672


EPSILON = 1e-06
ROPE_BASE = 1000042.0
CHUNKS = 1


def rotate_rows(values, head_size, first_pos):
    row_count = values.shape[0]
    shaped = values.reshape(row_count, -1, head_size)
    half_size = head_size // 2
    frequency = ROPE_BASE ** (jnp.arange(half_size, dtype=jnp.float32) * (-2.0 / head_size))
    positions = (first_pos + jnp.arange(row_count, dtype=jnp.int32)).astype(jnp.float32)
    angles = positions[:, None] * frequency[None, :]
    cosine_table = jnp.cos(angles)[:, None, :]
    sine_table = jnp.sin(angles)[:, None, :]
    first_half = shaped[..., :half_size]
    second_half = shaped[..., half_size:]
    turned = jnp.concatenate(
        [
            first_half * cosine_table - second_half * sine_table,
            second_half * cosine_table + first_half * sine_table,
        ],
        axis=-1,
    )
    return turned.reshape(values.shape)


def normalize(rows_in, gain):
    widened = rows_in.astype(jnp.float32)
    inverse_rms = lax.rsqrt(jnp.mean(widened * widened, axis=-1, keepdims=True) + EPSILON)
    return (widened * inverse_rms * gain.astype(jnp.float32)).astype(jnp.bfloat16)


def attend(query_block, start_row, key_rows, value_rows, length):
    row_count = query_block.shape[0]
    scores = jnp.dot(query_block, key_rows.T, preferred_element_type=jnp.float32) * key_rows.shape[
        1
    ] ** (-0.5)
    query_pos = start_row + jnp.arange(row_count, dtype=jnp.int32)[:, None]
    key_pos = jnp.arange(key_rows.shape[0], dtype=jnp.int32)[None, :]
    allowed = (key_pos <= query_pos) & (key_pos < length)
    scores = jnp.where(allowed, scores, -jnp.inf)
    row_top = jnp.max(scores, axis=-1, keepdims=True)
    powered = jnp.exp(scores - row_top)
    weights = (powered / jnp.sum(powered, axis=-1, keepdims=True)).astype(jnp.bfloat16)
    return jnp.dot(weights, value_rows, preferred_element_type=jnp.float32).astype(jnp.bfloat16)


def to_request(received, shift_by):
    rolled = jnp.roll(received, -shift_by, axis=0)
    return jnp.swapaxes(rolled, 0, 1).reshape(-1, received.shape[2])


def from_request(request_rows, shift_by, source_count):
    shaped = request_rows.reshape(-1, source_count, request_rows.shape[1])
    return jnp.roll(jnp.swapaxes(shaped, 0, 1), shift_by, axis=0)


def ring_blocks(narrow, axis_name):
    count = lax.axis_size(axis_name)
    blocks = [narrow]
    for shift in range(1, count):
        perm = [(index, (index - shift) % count) for index in range(count)]
        blocks.append(lax.ppermute(narrow, axis_name, perm))
    return blocks


def project_blocks(blocks, gain, query_weight, keyval_weight, axis_name):
    position = lax.axis_index(axis_name)
    offset = position * blocks[0].shape[1]
    rows = jnp.concatenate(blocks, axis=1)
    normed = normalize(rows, jnp.roll(gain, -offset))
    queries = jnp.dot(
        normed, jnp.roll(query_weight, -offset, axis=0), preferred_element_type=jnp.float32
    )
    keyvals = jnp.dot(
        normed, jnp.roll(keyval_weight, -offset, axis=0), preferred_element_type=jnp.float32
    )
    return queries, keyvals


def ring_output(local_attention, output_weight, axis_name):
    count = lax.axis_size(axis_name)
    position = lax.axis_index(axis_name)
    width = output_weight.shape[1] // count
    rotated = jnp.roll(output_weight, -position * width, axis=1)
    stacked = jnp.transpose(rotated.reshape(rotated.shape[0], count, width), (1, 0, 2))
    parts = jnp.einsum(
        "id,kdc->kic", local_attention, stacked, preferred_element_type=jnp.float32
    ).astype(jnp.bfloat16)
    total = parts[0].astype(jnp.float32)
    for shift in range(1, count):
        perm = [(index, (index + shift) % count) for index in range(count)]
        total = total + lax.ppermute(parts[shift], axis_name, perm).astype(jnp.float32)
    return total.astype(jnp.bfloat16)


def body(
    hidden_in,
    norm_gain,
    query_weight,
    keyval_weight,
    output_weight,
    segment_ids,
    request_lengths,
    request_owner,
    cache_slots,
):
    source_count = lax.axis_size("seq")
    source_pos = lax.axis_index("seq")
    local_rows = hidden_in.shape[0]
    capacity = MAXLEN // source_count
    chunk_slots = capacity // CHUNKS
    chunk_rows = chunk_slots * source_count
    request_ids = jnp.arange(source_count, dtype=jnp.int32)
    starts = jnp.sum(
        jnp.where(request_ids[None, :] < request_ids[:, None], request_lengths[None, :], 0), axis=1
    )
    first_row = jnp.maximum((starts - source_pos + source_count - 1) // source_count, 0)
    owner_match = request_owner[None, :] == request_ids[:, None]
    send_first = jnp.sum(jnp.where(owner_match, first_row[None, :], 0), axis=1)
    send_start = jnp.sum(jnp.where(owner_match, starts[None, :], 0), axis=1)
    send_length = jnp.sum(jnp.where(owner_match, request_lengths[None, :], 0), axis=1)
    row_index = send_first[:, None] + jnp.arange(capacity, dtype=jnp.int32)[None, :]
    stream_pos = row_index * source_count + source_pos
    live_send = (
        (row_index < local_rows)
        & (stream_pos >= send_start[:, None])
        & (stream_pos < (send_start + send_length)[:, None])
    )
    local_ids = jnp.arange(local_rows, dtype=jnp.int32)
    select = (
        (row_index.reshape(-1)[:, None] == local_ids[None, :]) & live_send.reshape(-1)[:, None]
    ).astype(jnp.bfloat16)
    send_slot = jnp.sum(jnp.where(owner_match, cache_slots[None, :], 0), axis=1)
    own_start = lax.dynamic_index_in_dim(send_start, source_pos, 0, keepdims=False)
    own_length = lax.dynamic_index_in_dim(send_length, source_pos, 0, keepdims=False)
    own_slot = lax.dynamic_index_in_dim(send_slot, source_pos, 0, keepdims=False)
    shift_by = own_start % source_count
    picked = (
        jnp.dot(select, hidden_in, preferred_element_type=jnp.float32)
        .astype(jnp.bfloat16)
        .reshape(source_count, capacity, hidden_in.shape[1])
    )
    head_count = query_weight.shape[1] // HD
    per_group = HEADS // KV_HEADS
    block_count = keyval_weight.shape[1] // HD
    key_chunks = []
    value_chunks = []
    cached_chunks = []
    returned_chunks = []
    for chunk in range(CHUNKS):
        chunk_first = chunk * chunk_rows
        arrived = lax.all_to_all(
            picked[:, chunk * chunk_slots : (chunk + 1) * chunk_slots],
            "seq",
            split_axis=0,
            concat_axis=0,
            tiled=True,
        )
        narrow_rows = to_request(arrived, shift_by)
        queries, keyvals = project_blocks(
            ring_blocks(narrow_rows, "tensor"), norm_gain, query_weight, keyval_weight, "tensor"
        )
        rotated_query = rotate_rows(queries, HD, chunk_first).astype(jnp.bfloat16)
        own_blocks = []
        for block_index in range(block_count):
            plain_block = keyvals[:, block_index * HD : (block_index + 1) * HD]
            if block_index % 2 == 0:
                own_blocks.append(rotate_rows(plain_block, HD, chunk_first).astype(jnp.bfloat16))
            else:
                own_blocks.append(plain_block.astype(jnp.bfloat16))
        own_cached = jnp.concatenate(own_blocks, axis=1)
        cached_chunks.append(own_cached)
        key_chunks.append(own_cached[:, 0:HD])
        value_chunks.append(own_cached[:, HD : 2 * HD])
        key_rows = jnp.concatenate(key_chunks, axis=0)
        value_rows = jnp.concatenate(value_chunks, axis=0)
        head_outputs = []
        for head_index in range(head_count):
            head_outputs.append(
                attend(
                    rotated_query[:, head_index * HD : (head_index + 1) * HD],
                    chunk_first,
                    key_rows,
                    value_rows,
                    own_length,
                )
            )
        attention_rows = jnp.concatenate(head_outputs, axis=1)
        outgoing = from_request(attention_rows, shift_by, source_count)
        returned_chunks.append(
            lax.all_to_all(outgoing, "seq", split_axis=0, concat_axis=0, tiled=True)
        )
    returned = jnp.concatenate(returned_chunks, axis=1)
    flattened = returned.reshape(-1, returned.shape[2])
    local_attention = lax.dot_general(
        select, flattened, (((0,), (0,)), ((), ())), preferred_element_type=jnp.float32
    ).astype(jnp.bfloat16)
    filled_rows = min(-(-FILLED // source_count), local_rows)
    attended = ring_output(local_attention[:filled_rows], output_weight, "tensor")
    if filled_rows < local_rows:
        attended = jnp.concatenate(
            [attended, jnp.zeros((local_rows - filled_rows, attended.shape[1]), attended.dtype)],
            axis=0,
        )
    all_cached = jnp.concatenate(cached_chunks, axis=0)
    slot_ids = jnp.arange(SLOTS_DEV, dtype=jnp.int32)
    cache_table = jnp.where(
        (slot_ids == own_slot)[:, None, None], all_cached[None], jnp.zeros((), jnp.bfloat16)
    )
    return (attended, cache_table)


def solution(mesh):
    in_specs = (
        P("seq", "tensor"),
        P(),
        P(None, "tensor"),
        P(None, "tensor"),
        P("tensor", None),
        P("seq"),
        P(),
        P(),
        P(),
    )
    out_specs = (P("seq", "tensor"), P("seq", None, "tensor"))
    return jax.shard_map(body, mesh=mesh, in_specs=in_specs, out_specs=out_specs, check_vma=False)
```

```python
import jax
import jax.numpy as jnp
from jax import lax
from jax.sharding import PartitionSpec as P

HEADS = 8
KV_HEADS = 4
HD = 256
SLOTS_DEV = 2
MAXLEN = 512
FILLED = 28672


EPSILON = 1e-06
ROPE_BASE = 1000042.0
CHUNKS = 1


def rotate_rows(values, head_size, first_pos):
    row_count = values.shape[0]
    shaped = values.reshape(row_count, -1, head_size)
    half_size = head_size // 2
    frequency = ROPE_BASE ** (jnp.arange(half_size, dtype=jnp.float32) * (-2.0 / head_size))
    positions = (first_pos + jnp.arange(row_count, dtype=jnp.int32)).astype(jnp.float32)
    angles = positions[:, None] * frequency[None, :]
    cosine_table = jnp.cos(angles)[:, None, :]
    sine_table = jnp.sin(angles)[:, None, :]
    first_half = shaped[..., :half_size]
    second_half = shaped[..., half_size:]
    turned = jnp.concatenate(
        [
            first_half * cosine_table - second_half * sine_table,
            second_half * cosine_table + first_half * sine_table,
        ],
        axis=-1,
    )
    return turned.reshape(values.shape)


def normalize(rows_in, gain):
    widened = rows_in.astype(jnp.float32)
    inverse_rms = lax.rsqrt(jnp.mean(widened * widened, axis=-1, keepdims=True) + EPSILON)
    return (widened * inverse_rms * gain.astype(jnp.float32)).astype(jnp.bfloat16)


def attend(query_block, start_row, key_rows, value_rows, length):
    row_count = query_block.shape[0]
    scores = jnp.dot(query_block, key_rows.T, preferred_element_type=jnp.float32) * key_rows.shape[
        1
    ] ** (-0.5)
    query_pos = start_row + jnp.arange(row_count, dtype=jnp.int32)[:, None]
    key_pos = jnp.arange(key_rows.shape[0], dtype=jnp.int32)[None, :]
    allowed = (key_pos <= query_pos) & (key_pos < length)
    scores = jnp.where(allowed, scores, -jnp.inf)
    row_top = jnp.max(scores, axis=-1, keepdims=True)
    powered = jnp.exp(scores - row_top)
    weights = (powered / jnp.sum(powered, axis=-1, keepdims=True)).astype(jnp.bfloat16)
    return jnp.dot(weights, value_rows, preferred_element_type=jnp.float32).astype(jnp.bfloat16)


def to_request(received, shift_by):
    rolled = jnp.roll(received, -shift_by, axis=0)
    return jnp.swapaxes(rolled, 0, 1).reshape(-1, received.shape[2])


def from_request(request_rows, shift_by, source_count):
    shaped = request_rows.reshape(-1, source_count, request_rows.shape[1])
    return jnp.roll(jnp.swapaxes(shaped, 0, 1), shift_by, axis=0)


def ring_blocks(narrow, axis_name):
    count = lax.axis_size(axis_name)
    blocks = [narrow]
    for shift in range(1, count):
        perm = [(index, (index - shift) % count) for index in range(count)]
        blocks.append(lax.ppermute(narrow, axis_name, perm))
    return blocks


def project_blocks(blocks, gain, query_weight, keyval_weight):
    rows = jnp.concatenate(blocks, axis=1)
    normed = normalize(rows, gain)
    queries = jnp.dot(normed, query_weight, preferred_element_type=jnp.float32)
    keyvals = jnp.dot(normed, keyval_weight, preferred_element_type=jnp.float32)
    return queries, keyvals


def ring_output(local_attention, output_weight, axis_name):
    count = lax.axis_size(axis_name)
    position = lax.axis_index(axis_name)
    width = output_weight.shape[1] // count
    rotated = jnp.roll(output_weight, -position * width, axis=1)
    stacked = jnp.transpose(rotated.reshape(rotated.shape[0], count, width), (1, 0, 2))
    parts = jnp.einsum(
        "id,kdc->kic", local_attention, stacked, preferred_element_type=jnp.float32
    ).astype(jnp.bfloat16)
    total = parts[0].astype(jnp.float32)
    for shift in range(1, count):
        perm = [(index, (index + shift) % count) for index in range(count)]
        total = total + lax.ppermute(parts[shift], axis_name, perm).astype(jnp.float32)
    return total.astype(jnp.bfloat16)


def body(
    hidden_in,
    norm_gain,
    query_weight,
    keyval_weight,
    output_weight,
    segment_ids,
    request_lengths,
    request_owner,
    cache_slots,
):
    source_count = lax.axis_size("seq")
    source_pos = lax.axis_index("seq")
    local_rows = hidden_in.shape[0]
    capacity = MAXLEN // source_count
    chunk_slots = capacity // CHUNKS
    chunk_rows = chunk_slots * source_count
    request_ids = jnp.arange(source_count, dtype=jnp.int32)
    starts = jnp.sum(
        jnp.where(request_ids[None, :] < request_ids[:, None], request_lengths[None, :], 0), axis=1
    )
    first_row = jnp.maximum((starts - source_pos + source_count - 1) // source_count, 0)
    owner_match = request_owner[None, :] == request_ids[:, None]
    send_first = jnp.sum(jnp.where(owner_match, first_row[None, :], 0), axis=1)
    send_start = jnp.sum(jnp.where(owner_match, starts[None, :], 0), axis=1)
    send_length = jnp.sum(jnp.where(owner_match, request_lengths[None, :], 0), axis=1)
    row_index = send_first[:, None] + jnp.arange(capacity, dtype=jnp.int32)[None, :]
    stream_pos = row_index * source_count + source_pos
    live_send = (
        (row_index < local_rows)
        & (stream_pos >= send_start[:, None])
        & (stream_pos < (send_start + send_length)[:, None])
    )
    local_ids = jnp.arange(local_rows, dtype=jnp.int32)
    select = (
        (row_index.reshape(-1)[:, None] == local_ids[None, :]) & live_send.reshape(-1)[:, None]
    ).astype(jnp.bfloat16)
    send_slot = jnp.sum(jnp.where(owner_match, cache_slots[None, :], 0), axis=1)
    own_start = lax.dynamic_index_in_dim(send_start, source_pos, 0, keepdims=False)
    own_length = lax.dynamic_index_in_dim(send_length, source_pos, 0, keepdims=False)
    own_slot = lax.dynamic_index_in_dim(send_slot, source_pos, 0, keepdims=False)
    shift_by = own_start % source_count
    picked = (
        jnp.dot(select, hidden_in, preferred_element_type=jnp.float32)
        .astype(jnp.bfloat16)
        .reshape(source_count, capacity, hidden_in.shape[1])
    )
    head_count = query_weight.shape[1] // HD
    per_group = HEADS // KV_HEADS
    block_count = keyval_weight.shape[1] // HD
    key_chunks = []
    value_chunks = []
    cached_chunks = []
    returned_chunks = []
    for chunk in range(CHUNKS):
        chunk_first = chunk * chunk_rows
        arrived = lax.all_to_all(
            picked[:, chunk * chunk_slots : (chunk + 1) * chunk_slots],
            "seq",
            split_axis=0,
            concat_axis=0,
            tiled=True,
        )
        tensor_offset = lax.axis_index("tensor") * arrived.shape[2]
        arrived, gain_rolled, query_rolled, keyval_rolled = lax.optimization_barrier(
            (
                arrived,
                jnp.roll(norm_gain, -tensor_offset),
                jnp.roll(query_weight, -tensor_offset, axis=0),
                jnp.roll(keyval_weight, -tensor_offset, axis=0),
            )
        )
        narrow_rows = to_request(arrived, shift_by)
        queries, keyvals = project_blocks(
            ring_blocks(narrow_rows, "tensor"), gain_rolled, query_rolled, keyval_rolled
        )
        rotated_query = rotate_rows(queries, HD, chunk_first).astype(jnp.bfloat16)
        own_blocks = []
        for block_index in range(block_count):
            plain_block = keyvals[:, block_index * HD : (block_index + 1) * HD]
            if block_index % 2 == 0:
                own_blocks.append(rotate_rows(plain_block, HD, chunk_first).astype(jnp.bfloat16))
            else:
                own_blocks.append(plain_block.astype(jnp.bfloat16))
        own_cached = jnp.concatenate(own_blocks, axis=1)
        cached_chunks.append(own_cached)
        key_chunks.append(own_cached[:, 0:HD])
        value_chunks.append(own_cached[:, HD : 2 * HD])
        key_rows = jnp.concatenate(key_chunks, axis=0)
        value_rows = jnp.concatenate(value_chunks, axis=0)
        head_outputs = []
        for head_index in range(head_count):
            head_outputs.append(
                attend(
                    rotated_query[:, head_index * HD : (head_index + 1) * HD],
                    chunk_first,
                    key_rows,
                    value_rows,
                    own_length,
                )
            )
        attention_rows = jnp.concatenate(head_outputs, axis=1)
        outgoing = from_request(attention_rows, shift_by, source_count)
        returned_chunks.append(
            lax.all_to_all(outgoing, "seq", split_axis=0, concat_axis=0, tiled=True)
        )
    returned = jnp.concatenate(returned_chunks, axis=1)
    flattened = returned.reshape(-1, returned.shape[2])
    local_attention = lax.dot_general(
        select, flattened, (((0,), (0,)), ((), ())), preferred_element_type=jnp.float32
    ).astype(jnp.bfloat16)
    filled_rows = min(-(-FILLED // source_count), local_rows)
    attended = ring_output(local_attention[:filled_rows], output_weight, "tensor")
    if filled_rows < local_rows:
        attended = jnp.concatenate(
            [attended, jnp.zeros((local_rows - filled_rows, attended.shape[1]), attended.dtype)],
            axis=0,
        )
    all_cached = jnp.concatenate(cached_chunks, axis=0)
    slot_ids = jnp.arange(SLOTS_DEV, dtype=jnp.int32)
    cache_table = jnp.where(
        (slot_ids == own_slot)[:, None, None], all_cached[None], jnp.zeros((), jnp.bfloat16)
    )
    return (attended, cache_table)


def solution(mesh):
    in_specs = (
        P("seq", "tensor"),
        P(),
        P(None, "tensor"),
        P(None, "tensor"),
        P("tensor", None),
        P("seq"),
        P(),
        P(),
        P(),
    )
    out_specs = (P("seq", "tensor"), P("seq", None, "tensor"))
    return jax.shard_map(body, mesh=mesh, in_specs=in_specs, out_specs=out_specs, check_vma=False)
```

```python
import jax
import jax.numpy as jnp
from jax import lax
from jax.sharding import PartitionSpec as P

HEADS = 8
KV_HEADS = 4
HD = 256
SLOTS_DEV = 2
MAXLEN = 512
FILLED = 28672


EPSILON = 1e-06
ROPE_BASE = 1000042.0
CHUNKS = 1


def rotate_rows(values, head_size, first_pos):
    row_count = values.shape[0]
    shaped = values.reshape(row_count, -1, head_size)
    half_size = head_size // 2
    frequency = ROPE_BASE ** (jnp.arange(half_size, dtype=jnp.float32) * (-2.0 / head_size))
    positions = (first_pos + jnp.arange(row_count, dtype=jnp.int32)).astype(jnp.float32)
    angles = positions[:, None] * frequency[None, :]
    cosine_table = jnp.cos(angles)[:, None, :]
    sine_table = jnp.sin(angles)[:, None, :]
    first_half = shaped[..., :half_size]
    second_half = shaped[..., half_size:]
    turned = jnp.concatenate(
        [
            first_half * cosine_table - second_half * sine_table,
            second_half * cosine_table + first_half * sine_table,
        ],
        axis=-1,
    )
    return turned.reshape(values.shape)


def normalize(rows_in, gain):
    widened = rows_in.astype(jnp.float32)
    inverse_rms = lax.rsqrt(jnp.mean(widened * widened, axis=-1, keepdims=True) + EPSILON)
    return (widened * inverse_rms * gain.astype(jnp.float32)).astype(jnp.bfloat16)


def attend(query_block, start_row, key_rows, value_rows, length):
    row_count = query_block.shape[0]
    scores = jnp.dot(query_block, key_rows.T, preferred_element_type=jnp.float32) * key_rows.shape[
        1
    ] ** (-0.5)
    query_pos = start_row + jnp.arange(row_count, dtype=jnp.int32)[:, None]
    key_pos = jnp.arange(key_rows.shape[0], dtype=jnp.int32)[None, :]
    allowed = (key_pos <= query_pos) & (key_pos < length)
    scores = jnp.where(allowed, scores, -jnp.inf)
    row_top = jnp.max(scores, axis=-1, keepdims=True)
    powered = jnp.exp(scores - row_top)
    weights = (powered / jnp.sum(powered, axis=-1, keepdims=True)).astype(jnp.bfloat16)
    return jnp.dot(weights, value_rows, preferred_element_type=jnp.float32).astype(jnp.bfloat16)


def to_request(received, shift_by):
    rolled = jnp.roll(received, -shift_by, axis=0)
    return jnp.swapaxes(rolled, 0, 1).reshape(-1, received.shape[2])


def from_request(request_rows, shift_by, source_count):
    shaped = request_rows.reshape(-1, source_count, request_rows.shape[1])
    return jnp.roll(jnp.swapaxes(shaped, 0, 1), shift_by, axis=0)


def ring_blocks(narrow, axis_name):
    count = lax.axis_size(axis_name)
    blocks = [narrow]
    for shift in range(1, count):
        perm = [(index, (index - shift) % count) for index in range(count)]
        blocks.append(lax.ppermute(narrow, axis_name, perm))
    return blocks


def project_blocks(blocks, gain, joint_weight, query_width):
    rows = jnp.concatenate(blocks, axis=1)
    normed = normalize(rows, gain)
    joint = jnp.dot(normed, joint_weight, preferred_element_type=jnp.float32)
    return joint[:, :query_width], joint[:, query_width:]


def ring_output(local_attention, output_weight, axis_name):
    count = lax.axis_size(axis_name)
    position = lax.axis_index(axis_name)
    width = output_weight.shape[1] // count
    rotated = jnp.roll(output_weight, -position * width, axis=1)
    stacked = jnp.transpose(rotated.reshape(rotated.shape[0], count, width), (1, 0, 2))
    parts = jnp.einsum(
        "id,kdc->kic", local_attention, stacked, preferred_element_type=jnp.float32
    ).astype(jnp.bfloat16)
    total = parts[0].astype(jnp.float32)
    for shift in range(1, count):
        perm = [(index, (index + shift) % count) for index in range(count)]
        total = total + lax.ppermute(parts[shift], axis_name, perm).astype(jnp.float32)
    return total.astype(jnp.bfloat16)


def body(
    hidden_in,
    norm_gain,
    query_weight,
    keyval_weight,
    output_weight,
    segment_ids,
    request_lengths,
    request_owner,
    cache_slots,
):
    source_count = lax.axis_size("seq")
    source_pos = lax.axis_index("seq")
    local_rows = hidden_in.shape[0]
    capacity = MAXLEN // source_count
    chunk_slots = capacity // CHUNKS
    chunk_rows = chunk_slots * source_count
    request_ids = jnp.arange(source_count, dtype=jnp.int32)
    starts = jnp.sum(
        jnp.where(request_ids[None, :] < request_ids[:, None], request_lengths[None, :], 0), axis=1
    )
    first_row = jnp.maximum((starts - source_pos + source_count - 1) // source_count, 0)
    owner_match = request_owner[None, :] == request_ids[:, None]
    send_first = jnp.sum(jnp.where(owner_match, first_row[None, :], 0), axis=1)
    send_start = jnp.sum(jnp.where(owner_match, starts[None, :], 0), axis=1)
    send_length = jnp.sum(jnp.where(owner_match, request_lengths[None, :], 0), axis=1)
    row_index = send_first[:, None] + jnp.arange(capacity, dtype=jnp.int32)[None, :]
    stream_pos = row_index * source_count + source_pos
    live_send = (
        (row_index < local_rows)
        & (stream_pos >= send_start[:, None])
        & (stream_pos < (send_start + send_length)[:, None])
    )
    local_ids = jnp.arange(local_rows, dtype=jnp.int32)
    select = (
        (row_index.reshape(-1)[:, None] == local_ids[None, :]) & live_send.reshape(-1)[:, None]
    ).astype(jnp.bfloat16)
    send_slot = jnp.sum(jnp.where(owner_match, cache_slots[None, :], 0), axis=1)
    own_start = lax.dynamic_index_in_dim(send_start, source_pos, 0, keepdims=False)
    own_length = lax.dynamic_index_in_dim(send_length, source_pos, 0, keepdims=False)
    own_slot = lax.dynamic_index_in_dim(send_slot, source_pos, 0, keepdims=False)
    shift_by = own_start % source_count
    picked = (
        jnp.dot(select, hidden_in, preferred_element_type=jnp.float32)
        .astype(jnp.bfloat16)
        .reshape(source_count, capacity, hidden_in.shape[1])
    )
    head_count = query_weight.shape[1] // HD
    per_group = HEADS // KV_HEADS
    block_count = keyval_weight.shape[1] // HD
    key_chunks = []
    value_chunks = []
    cached_chunks = []
    returned_chunks = []
    for chunk in range(CHUNKS):
        chunk_first = chunk * chunk_rows
        arrived = lax.all_to_all(
            picked[:, chunk * chunk_slots : (chunk + 1) * chunk_slots],
            "seq",
            split_axis=0,
            concat_axis=0,
            tiled=True,
        )
        tensor_offset = lax.axis_index("tensor") * arrived.shape[2]
        arrived, gain_rolled, joint_rolled = lax.optimization_barrier(
            (
                arrived,
                jnp.roll(norm_gain, -tensor_offset),
                jnp.roll(
                    jnp.concatenate([query_weight, keyval_weight], axis=1), -tensor_offset, axis=0
                ),
            )
        )
        narrow_rows = to_request(arrived, shift_by)
        queries, keyvals = project_blocks(
            ring_blocks(narrow_rows, "tensor"), gain_rolled, joint_rolled, query_weight.shape[1]
        )
        rotated_query = rotate_rows(queries, HD, chunk_first).astype(jnp.bfloat16)
        own_blocks = []
        for block_index in range(block_count):
            plain_block = keyvals[:, block_index * HD : (block_index + 1) * HD]
            if block_index % 2 == 0:
                own_blocks.append(rotate_rows(plain_block, HD, chunk_first).astype(jnp.bfloat16))
            else:
                own_blocks.append(plain_block.astype(jnp.bfloat16))
        own_cached = jnp.concatenate(own_blocks, axis=1)
        cached_chunks.append(own_cached)
        key_chunks.append(own_cached[:, 0:HD])
        value_chunks.append(own_cached[:, HD : 2 * HD])
        key_rows = jnp.concatenate(key_chunks, axis=0)
        value_rows = jnp.concatenate(value_chunks, axis=0)
        head_outputs = []
        for head_index in range(head_count):
            head_outputs.append(
                attend(
                    rotated_query[:, head_index * HD : (head_index + 1) * HD],
                    chunk_first,
                    key_rows,
                    value_rows,
                    own_length,
                )
            )
        attention_rows = jnp.concatenate(head_outputs, axis=1)
        outgoing = from_request(attention_rows, shift_by, source_count)
        returned_chunks.append(
            lax.all_to_all(outgoing, "seq", split_axis=0, concat_axis=0, tiled=True)
        )
    returned = jnp.concatenate(returned_chunks, axis=1)
    flattened = returned.reshape(-1, returned.shape[2])
    local_attention = lax.dot_general(
        select, flattened, (((0,), (0,)), ((), ())), preferred_element_type=jnp.float32
    ).astype(jnp.bfloat16)
    filled_rows = min(-(-FILLED // source_count), local_rows)
    attended = ring_output(local_attention[:filled_rows], output_weight, "tensor")
    if filled_rows < local_rows:
        attended = jnp.concatenate(
            [attended, jnp.zeros((local_rows - filled_rows, attended.shape[1]), attended.dtype)],
            axis=0,
        )
    all_cached = jnp.concatenate(cached_chunks, axis=0)
    slot_ids = jnp.arange(SLOTS_DEV, dtype=jnp.int32)
    cache_table = jnp.where(
        (slot_ids == own_slot)[:, None, None], all_cached[None], jnp.zeros((), jnp.bfloat16)
    )
    return (attended, cache_table)


def solution(mesh):
    in_specs = (
        P("seq", "tensor"),
        P(),
        P(None, "tensor"),
        P(None, "tensor"),
        P("tensor", None),
        P("seq"),
        P(),
        P(),
        P(),
    )
    out_specs = (P("seq", "tensor"), P("seq", None, "tensor"))
    return jax.shard_map(body, mesh=mesh, in_specs=in_specs, out_specs=out_specs, check_vma=False)
```

```python
import jax
import jax.numpy as jnp
from jax import lax
from jax.sharding import PartitionSpec as P

HEADS = 8
KV_HEADS = 4
HD = 256
SLOTS_DEV = 2
MAXLEN = 512
FILLED = 28672


EPSILON = 1e-06
ROPE_BASE = 1000042.0
CHUNKS = 1


def rotate_rows(values, head_size, first_pos):
    row_count = values.shape[0]
    shaped = values.reshape(row_count, -1, head_size)
    half_size = head_size // 2
    frequency = ROPE_BASE ** (jnp.arange(half_size, dtype=jnp.float32) * (-2.0 / head_size))
    positions = (first_pos + jnp.arange(row_count, dtype=jnp.int32)).astype(jnp.float32)
    angles = positions[:, None] * frequency[None, :]
    cosine_table = jnp.cos(angles)[:, None, :]
    sine_table = jnp.sin(angles)[:, None, :]
    first_half = shaped[..., :half_size]
    second_half = shaped[..., half_size:]
    turned = jnp.concatenate(
        [
            first_half * cosine_table - second_half * sine_table,
            second_half * cosine_table + first_half * sine_table,
        ],
        axis=-1,
    )
    return turned.reshape(values.shape)


def normalize(rows_in, gain):
    widened = rows_in.astype(jnp.float32)
    inverse_rms = lax.rsqrt(jnp.mean(widened * widened, axis=-1, keepdims=True) + EPSILON)
    return (widened * inverse_rms * gain.astype(jnp.float32)).astype(jnp.bfloat16)


def attend(query_block, start_row, key_rows, value_rows, length):
    row_count = query_block.shape[0]
    scores = jnp.dot(query_block, key_rows.T, preferred_element_type=jnp.float32) * key_rows.shape[
        1
    ] ** (-0.5)
    query_pos = start_row + jnp.arange(row_count, dtype=jnp.int32)[:, None]
    key_pos = jnp.arange(key_rows.shape[0], dtype=jnp.int32)[None, :]
    allowed = (key_pos <= query_pos) & (key_pos < length)
    scores = jnp.where(allowed, scores, -jnp.inf)
    row_top = jnp.max(scores, axis=-1, keepdims=True)
    powered = jnp.exp(scores - row_top)
    weights = (powered / jnp.sum(powered, axis=-1, keepdims=True)).astype(jnp.bfloat16)
    return jnp.dot(weights, value_rows, preferred_element_type=jnp.float32).astype(jnp.bfloat16)


def attend_rows(query_block, query_pos, key_rows, value_rows, length):
    scores = jnp.dot(query_block, key_rows.T, preferred_element_type=jnp.float32) * key_rows.shape[
        1
    ] ** (-0.5)
    key_pos = jnp.arange(key_rows.shape[0], dtype=jnp.int32)[None, :]
    allowed = (key_pos <= query_pos[:, None]) & (key_pos < length)
    scores = jnp.where(allowed, scores, -jnp.inf)
    row_top = jnp.max(scores, axis=-1, keepdims=True)
    powered = jnp.exp(scores - row_top)
    weights = (powered / jnp.sum(powered, axis=-1, keepdims=True)).astype(jnp.bfloat16)
    return jnp.dot(weights, value_rows, preferred_element_type=jnp.float32).astype(jnp.bfloat16)


def to_request(received, shift_by):
    rolled = jnp.roll(received, -shift_by, axis=0)
    return jnp.swapaxes(rolled, 0, 1).reshape(-1, received.shape[2])


def from_request(request_rows, shift_by, source_count):
    shaped = request_rows.reshape(-1, source_count, request_rows.shape[1])
    return jnp.roll(jnp.swapaxes(shaped, 0, 1), shift_by, axis=0)


def ring_blocks(narrow, axis_name):
    count = lax.axis_size(axis_name)
    blocks = [narrow]
    for shift in range(1, count):
        perm = [(index, (index - shift) % count) for index in range(count)]
        blocks.append(lax.ppermute(narrow, axis_name, perm))
    return blocks


def project_blocks(blocks, gain, query_weight, keyval_weight):
    rows = jnp.concatenate(blocks, axis=1)
    normed = normalize(rows, gain)
    queries = jnp.dot(normed, query_weight, preferred_element_type=jnp.float32)
    keyvals = jnp.dot(normed, keyval_weight, preferred_element_type=jnp.float32)
    return queries, keyvals


def ring_output(local_attention, output_weight, axis_name):
    count = lax.axis_size(axis_name)
    position = lax.axis_index(axis_name)
    width = output_weight.shape[1] // count
    rotated = jnp.roll(output_weight, -position * width, axis=1)
    stacked = jnp.transpose(rotated.reshape(rotated.shape[0], count, width), (1, 0, 2))
    parts = jnp.einsum(
        "id,kdc->kic", local_attention, stacked, preferred_element_type=jnp.float32
    ).astype(jnp.bfloat16)
    total = parts[0].astype(jnp.float32)
    for shift in range(1, count):
        perm = [(index, (index + shift) % count) for index in range(count)]
        total = total + lax.ppermute(parts[shift], axis_name, perm).astype(jnp.float32)
    return total.astype(jnp.bfloat16)


def body(
    hidden_in,
    norm_gain,
    query_weight,
    keyval_weight,
    output_weight,
    segment_ids,
    request_lengths,
    request_owner,
    cache_slots,
):
    source_count = lax.axis_size("seq")
    source_pos = lax.axis_index("seq")
    local_rows = hidden_in.shape[0]
    capacity = MAXLEN // source_count
    chunk_slots = capacity // CHUNKS
    chunk_rows = chunk_slots * source_count
    request_ids = jnp.arange(source_count, dtype=jnp.int32)
    starts = jnp.sum(
        jnp.where(request_ids[None, :] < request_ids[:, None], request_lengths[None, :], 0), axis=1
    )
    first_row = jnp.maximum((starts - source_pos + source_count - 1) // source_count, 0)
    owner_match = request_owner[None, :] == request_ids[:, None]
    send_first = jnp.sum(jnp.where(owner_match, first_row[None, :], 0), axis=1)
    send_start = jnp.sum(jnp.where(owner_match, starts[None, :], 0), axis=1)
    send_length = jnp.sum(jnp.where(owner_match, request_lengths[None, :], 0), axis=1)
    row_index = send_first[:, None] + jnp.arange(capacity, dtype=jnp.int32)[None, :]
    stream_pos = row_index * source_count + source_pos
    live_send = (
        (row_index < local_rows)
        & (stream_pos >= send_start[:, None])
        & (stream_pos < (send_start + send_length)[:, None])
    )
    local_ids = jnp.arange(local_rows, dtype=jnp.int32)
    select = (
        (row_index.reshape(-1)[:, None] == local_ids[None, :]) & live_send.reshape(-1)[:, None]
    ).astype(jnp.bfloat16)
    send_slot = jnp.sum(jnp.where(owner_match, cache_slots[None, :], 0), axis=1)
    own_start = lax.dynamic_index_in_dim(send_start, source_pos, 0, keepdims=False)
    own_length = lax.dynamic_index_in_dim(send_length, source_pos, 0, keepdims=False)
    own_slot = lax.dynamic_index_in_dim(send_slot, source_pos, 0, keepdims=False)
    shift_by = own_start % source_count
    picked = (
        jnp.dot(select, hidden_in, preferred_element_type=jnp.float32)
        .astype(jnp.bfloat16)
        .reshape(source_count, capacity, hidden_in.shape[1])
    )
    head_count = query_weight.shape[1] // HD
    per_group = HEADS // KV_HEADS
    block_count = keyval_weight.shape[1] // HD
    key_chunks = []
    value_chunks = []
    cached_chunks = []
    returned_chunks = []
    for chunk in range(CHUNKS):
        chunk_first = chunk * chunk_rows
        arrived = lax.all_to_all(
            picked[:, chunk * chunk_slots : (chunk + 1) * chunk_slots],
            "seq",
            split_axis=0,
            concat_axis=0,
            tiled=True,
        )
        tensor_offset = lax.axis_index("tensor") * arrived.shape[2]
        arrived, gain_rolled, query_rolled, keyval_rolled = lax.optimization_barrier(
            (
                arrived,
                jnp.roll(norm_gain, -tensor_offset),
                jnp.roll(query_weight, -tensor_offset, axis=0),
                jnp.roll(keyval_weight, -tensor_offset, axis=0),
            )
        )
        narrow_rows = to_request(arrived, shift_by)
        queries, keyvals = project_blocks(
            ring_blocks(narrow_rows, "tensor"), gain_rolled, query_rolled, keyval_rolled
        )
        rotated_query = rotate_rows(queries, HD, chunk_first).astype(jnp.bfloat16)
        own_blocks = []
        for block_index in range(block_count):
            plain_block = keyvals[:, block_index * HD : (block_index + 1) * HD]
            if block_index % 2 == 0:
                own_blocks.append(rotate_rows(plain_block, HD, chunk_first).astype(jnp.bfloat16))
            else:
                own_blocks.append(plain_block.astype(jnp.bfloat16))
        own_cached = jnp.concatenate(own_blocks, axis=1)
        cached_chunks.append(own_cached)
        key_chunks.append(own_cached[:, 0:HD])
        value_chunks.append(own_cached[:, HD : 2 * HD])
        key_rows = jnp.concatenate(key_chunks, axis=0)
        value_rows = jnp.concatenate(value_chunks, axis=0)
        stacked_query = jnp.concatenate(
            [rotated_query[:, head_index * HD : (head_index + 1) * HD] for head_index in range(head_count)],
            axis=0,
        )
        if head_count == per_group:
            stacked_out = attend_rows(
                stacked_query, jnp.tile(chunk_first + jnp.arange(chunk_rows, dtype=jnp.int32), head_count),
                key_rows, value_rows, own_length,
            )
            head_outputs = [
                stacked_out[head_index * chunk_rows : (head_index + 1) * chunk_rows]
                for head_index in range(head_count)
            ]
        else:
            head_outputs = [
                attend(
                    rotated_query[:, head_index * HD : (head_index + 1) * HD],
                    chunk_first,
                    key_rows,
                    value_rows,
                    own_length,
                )
                for head_index in range(head_count)
            ]
        attention_rows = jnp.concatenate(head_outputs, axis=1)
        outgoing = from_request(attention_rows, shift_by, source_count)
        returned_chunks.append(
            lax.all_to_all(outgoing, "seq", split_axis=0, concat_axis=0, tiled=True)
        )
    returned = jnp.concatenate(returned_chunks, axis=1)
    flattened = returned.reshape(-1, returned.shape[2])
    local_attention = lax.dot_general(
        select, flattened, (((0,), (0,)), ((), ())), preferred_element_type=jnp.float32
    ).astype(jnp.bfloat16)
    filled_rows = min(-(-FILLED // source_count), local_rows)
    attended = ring_output(local_attention[:filled_rows], output_weight, "tensor")
    if filled_rows < local_rows:
        attended = jnp.concatenate(
            [attended, jnp.zeros((local_rows - filled_rows, attended.shape[1]), attended.dtype)],
            axis=0,
        )
    all_cached = jnp.concatenate(cached_chunks, axis=0)
    slot_ids = jnp.arange(SLOTS_DEV, dtype=jnp.int32)
    cache_table = jnp.where(
        (slot_ids == own_slot)[:, None, None], all_cached[None], jnp.zeros((), jnp.bfloat16)
    )
    return (attended, cache_table)


def solution(mesh):
    in_specs = (
        P("seq", "tensor"),
        P(),
        P(None, "tensor"),
        P(None, "tensor"),
        P("tensor", None),
        P("seq"),
        P(),
        P(),
        P(),
    )
    out_specs = (P("seq", "tensor"), P("seq", None, "tensor"))
    return jax.shard_map(body, mesh=mesh, in_specs=in_specs, out_specs=out_specs, check_vma=False)
```

```python
import jax
import jax.numpy as jnp
from jax import lax
from jax.sharding import PartitionSpec as P

HEADS = 8
KV_HEADS = 4
HD = 256
SLOTS_DEV = 2
MAXLEN = 512
FILLED = 28672


EPSILON = 1e-06
ROPE_BASE = 1000042.0
CHUNKS = 1


def rotate_rows(values, head_size, first_pos):
    row_count = values.shape[0]
    shaped = values.reshape(row_count, -1, head_size)
    half_size = head_size // 2
    frequency = ROPE_BASE ** (jnp.arange(half_size, dtype=jnp.float32) * (-2.0 / head_size))
    positions = (first_pos + jnp.arange(row_count, dtype=jnp.int32)).astype(jnp.float32)
    angles = positions[:, None] * frequency[None, :]
    cosine_table = jnp.cos(angles)[:, None, :]
    sine_table = jnp.sin(angles)[:, None, :]
    first_half = shaped[..., :half_size]
    second_half = shaped[..., half_size:]
    turned = jnp.concatenate(
        [
            first_half * cosine_table - second_half * sine_table,
            second_half * cosine_table + first_half * sine_table,
        ],
        axis=-1,
    )
    return turned.reshape(values.shape)


def normalize(rows_in, gain):
    widened = rows_in.astype(jnp.float32)
    inverse_rms = lax.rsqrt(jnp.mean(widened * widened, axis=-1, keepdims=True) + EPSILON)
    return (widened * inverse_rms * gain.astype(jnp.float32)).astype(jnp.bfloat16)


def attend(query_block, start_row, key_rows, value_rows, length):
    row_count = query_block.shape[0]
    scores = jnp.dot(query_block, key_rows.T, preferred_element_type=jnp.float32) * key_rows.shape[
        1
    ] ** (-0.5)
    query_pos = start_row + jnp.arange(row_count, dtype=jnp.int32)[:, None]
    key_pos = jnp.arange(key_rows.shape[0], dtype=jnp.int32)[None, :]
    allowed = (key_pos <= query_pos) & (key_pos < length)
    scores = jnp.where(allowed, scores, -jnp.inf)
    row_top = jnp.max(scores, axis=-1, keepdims=True)
    powered = jnp.exp(scores - row_top)
    weights = (powered / jnp.sum(powered, axis=-1, keepdims=True)).astype(jnp.bfloat16)
    return jnp.dot(weights, value_rows, preferred_element_type=jnp.float32).astype(jnp.bfloat16)


def attend_rows(query_block, query_pos, key_rows, value_rows, length):
    scores = jnp.dot(query_block, key_rows.T, preferred_element_type=jnp.float32) * key_rows.shape[
        1
    ] ** (-0.5)
    key_pos = jnp.arange(key_rows.shape[0], dtype=jnp.int32)[None, :]
    allowed = (key_pos <= query_pos[:, None]) & (key_pos < length)
    scores = jnp.where(allowed, scores, -jnp.inf)
    row_top = jnp.max(scores, axis=-1, keepdims=True)
    powered = jnp.exp(scores - row_top)
    weights = (powered / jnp.sum(powered, axis=-1, keepdims=True)).astype(jnp.bfloat16)
    return jnp.dot(weights, value_rows, preferred_element_type=jnp.float32).astype(jnp.bfloat16)


def to_request(received, shift_by):
    rolled = jnp.roll(received, -shift_by, axis=0)
    return jnp.swapaxes(rolled, 0, 1).reshape(-1, received.shape[2])


def from_request(request_rows, shift_by, source_count):
    shaped = request_rows.reshape(-1, source_count, request_rows.shape[1])
    return jnp.roll(jnp.swapaxes(shaped, 0, 1), shift_by, axis=0)


def ring_blocks(narrow, axis_name):
    count = lax.axis_size(axis_name)
    blocks = [narrow]
    for shift in range(1, count):
        perm = [(index, (index - shift) % count) for index in range(count)]
        blocks.append(lax.ppermute(narrow, axis_name, perm))
    return blocks


def project_blocks(blocks, gain, query_weight, keyval_weight):
    rows = jnp.concatenate(blocks, axis=1)
    normed = normalize(rows, gain)
    queries = jnp.dot(normed, query_weight, preferred_element_type=jnp.float32)
    keyvals = jnp.dot(normed, keyval_weight, preferred_element_type=jnp.float32)
    return queries, keyvals


def ring_output(local_attention, output_weight, axis_name, sent_rows):
    count = lax.axis_size(axis_name)
    position = lax.axis_index(axis_name)
    width = output_weight.shape[1] // count
    rotated = jnp.roll(output_weight, -position * width, axis=1)
    stacked = jnp.transpose(rotated.reshape(rotated.shape[0], count, width), (1, 0, 2))
    own = jnp.dot(
        local_attention, stacked[0], preferred_element_type=jnp.float32
    ).astype(jnp.bfloat16)
    parts = jnp.einsum(
        "id,kdc->kic", local_attention[:sent_rows], stacked[1:], preferred_element_type=jnp.float32
    ).astype(jnp.bfloat16)
    pad_rows = local_attention.shape[0] - sent_rows
    total = own.astype(jnp.float32)
    for shift in range(1, count):
        perm = [(index, (index + shift) % count) for index in range(count)]
        arrived = lax.ppermute(parts[shift - 1], axis_name, perm).astype(jnp.float32)
        total = total + jnp.pad(arrived, ((0, pad_rows), (0, 0)))
    return total.astype(jnp.bfloat16)


def body(
    hidden_in,
    norm_gain,
    query_weight,
    keyval_weight,
    output_weight,
    segment_ids,
    request_lengths,
    request_owner,
    cache_slots,
):
    source_count = lax.axis_size("seq")
    source_pos = lax.axis_index("seq")
    local_rows = hidden_in.shape[0]
    capacity = MAXLEN // source_count
    chunk_slots = capacity // CHUNKS
    chunk_rows = chunk_slots * source_count
    request_ids = jnp.arange(source_count, dtype=jnp.int32)
    starts = jnp.sum(
        jnp.where(request_ids[None, :] < request_ids[:, None], request_lengths[None, :], 0), axis=1
    )
    first_row = jnp.maximum((starts - source_pos + source_count - 1) // source_count, 0)
    owner_match = request_owner[None, :] == request_ids[:, None]
    send_first = jnp.sum(jnp.where(owner_match, first_row[None, :], 0), axis=1)
    send_start = jnp.sum(jnp.where(owner_match, starts[None, :], 0), axis=1)
    send_length = jnp.sum(jnp.where(owner_match, request_lengths[None, :], 0), axis=1)
    row_index = send_first[:, None] + jnp.arange(capacity, dtype=jnp.int32)[None, :]
    stream_pos = row_index * source_count + source_pos
    live_send = (
        (row_index < local_rows)
        & (stream_pos >= send_start[:, None])
        & (stream_pos < (send_start + send_length)[:, None])
    )
    local_ids = jnp.arange(local_rows, dtype=jnp.int32)
    select = (
        (row_index.reshape(-1)[:, None] == local_ids[None, :]) & live_send.reshape(-1)[:, None]
    ).astype(jnp.bfloat16)
    send_slot = jnp.sum(jnp.where(owner_match, cache_slots[None, :], 0), axis=1)
    own_start = lax.dynamic_index_in_dim(send_start, source_pos, 0, keepdims=False)
    own_length = lax.dynamic_index_in_dim(send_length, source_pos, 0, keepdims=False)
    own_slot = lax.dynamic_index_in_dim(send_slot, source_pos, 0, keepdims=False)
    shift_by = own_start % source_count
    picked = (
        jnp.dot(select, hidden_in, preferred_element_type=jnp.float32)
        .astype(jnp.bfloat16)
        .reshape(source_count, capacity, hidden_in.shape[1])
    )
    head_count = query_weight.shape[1] // HD
    per_group = HEADS // KV_HEADS
    block_count = keyval_weight.shape[1] // HD
    key_chunks = []
    value_chunks = []
    cached_chunks = []
    returned_chunks = []
    for chunk in range(CHUNKS):
        chunk_first = chunk * chunk_rows
        arrived = lax.all_to_all(
            picked[:, chunk * chunk_slots : (chunk + 1) * chunk_slots],
            "seq",
            split_axis=0,
            concat_axis=0,
            tiled=True,
        )
        tensor_offset = lax.axis_index("tensor") * arrived.shape[2]
        arrived, gain_rolled, query_rolled, keyval_rolled = lax.optimization_barrier(
            (
                arrived,
                jnp.roll(norm_gain, -tensor_offset),
                jnp.roll(query_weight, -tensor_offset, axis=0),
                jnp.roll(keyval_weight, -tensor_offset, axis=0),
            )
        )
        narrow_rows = to_request(arrived, shift_by)
        queries, keyvals = project_blocks(
            ring_blocks(narrow_rows, "tensor"), gain_rolled, query_rolled, keyval_rolled
        )
        rotated_query = rotate_rows(queries, HD, chunk_first).astype(jnp.bfloat16)
        own_blocks = []
        for block_index in range(block_count):
            plain_block = keyvals[:, block_index * HD : (block_index + 1) * HD]
            if block_index % 2 == 0:
                own_blocks.append(rotate_rows(plain_block, HD, chunk_first).astype(jnp.bfloat16))
            else:
                own_blocks.append(plain_block.astype(jnp.bfloat16))
        own_cached = jnp.concatenate(own_blocks, axis=1)
        cached_chunks.append(own_cached)
        key_chunks.append(own_cached[:, 0:HD])
        value_chunks.append(own_cached[:, HD : 2 * HD])
        key_rows = jnp.concatenate(key_chunks, axis=0)
        value_rows = jnp.concatenate(value_chunks, axis=0)
        stacked_query = jnp.concatenate(
            [rotated_query[:, head_index * HD : (head_index + 1) * HD] for head_index in range(head_count)],
            axis=0,
        )
        if head_count == per_group:
            stacked_out = attend_rows(
                stacked_query, jnp.tile(chunk_first + jnp.arange(chunk_rows, dtype=jnp.int32), head_count),
                key_rows, value_rows, own_length,
            )
            head_outputs = [
                stacked_out[head_index * chunk_rows : (head_index + 1) * chunk_rows]
                for head_index in range(head_count)
            ]
        else:
            head_outputs = [
                attend(
                    rotated_query[:, head_index * HD : (head_index + 1) * HD],
                    chunk_first,
                    key_rows,
                    value_rows,
                    own_length,
                )
                for head_index in range(head_count)
            ]
        attention_rows = jnp.concatenate(head_outputs, axis=1)
        outgoing = from_request(attention_rows, shift_by, source_count)
        returned_chunks.append(
            lax.all_to_all(outgoing, "seq", split_axis=0, concat_axis=0, tiled=True)
        )
    returned = jnp.concatenate(returned_chunks, axis=1)
    flattened = returned.reshape(-1, returned.shape[2])
    local_attention = lax.dot_general(
        select, flattened, (((0,), (0,)), ((), ())), preferred_element_type=jnp.float32
    ).astype(jnp.bfloat16)
    filled_rows = min(-(-FILLED // source_count), local_rows)
    attended = ring_output(local_attention, output_weight, "tensor", filled_rows)
    all_cached = jnp.concatenate(cached_chunks, axis=0)
    slot_ids = jnp.arange(SLOTS_DEV, dtype=jnp.int32)
    cache_table = jnp.where(
        (slot_ids == own_slot)[:, None, None], all_cached[None], jnp.zeros((), jnp.bfloat16)
    )
    return (attended, cache_table)


def solution(mesh):
    in_specs = (
        P("seq", "tensor"),
        P(),
        P(None, "tensor"),
        P(None, "tensor"),
        P("tensor", None),
        P("seq"),
        P(),
        P(),
        P(),
    )
    out_specs = (P("seq", "tensor"), P("seq", None, "tensor"))
    return jax.shard_map(body, mesh=mesh, in_specs=in_specs, out_specs=out_specs, check_vma=False)
```
